32 devices in a mesh: gx: 4 (over y, core), gy: 8 (over z, x).
Axes of the slice: x: 2, y: 2, z: 4, core: 2. Of those that a mesh axis runs over, the one named last changes fastest.
Arguments:
- old_states: bfloat16 [4096, 12, 128], P(('gx', 'gy')), may hold values from -6 to 6
- weight_tiles: bfloat16 [12288, 128, 128], P(('gx', 'gy')), may hold values from -0.5 to 0.5
- source_block: int32 [24576], P(('gx', 'gy')), may hold values from 0 to 127
- tile_index: int32 [24576], P(('gx', 'gy')), may hold values from 0 to 383
- dest_device: int32 [24576], P(('gx', 'gy')), may hold values from 0 to 31, as said below
- dest_block: int32 [24576], P(('gx', 'gy')), may hold values from 0 to 255
- send_count: int32 [32], P(('gx', 'gy')), may hold values from 576 to 768, as said below
- velocity: float32 [2, 1024, 1024], P(None, 'gx', 'gy'), may hold values from -4 to 4
Outputs:
- new_states: float32 [1024, 12, 1024], P('gx', None, 'gy')
The draws below stay inside these ranges and needn't reach their ends.
Inputs may be any that keep to these rules, and one draw needn't show every extreme that they name: `dest_device`: the live slots of a device name only the device itself and the devices of the tiles adjacent to its tile along gx and gy, diagonals included; among them no destination appears more than 192 times, and the device itself appears exactly 192 times. The live slots of a device are its first send_count slots; some device has all 768 live.
All inputs are finite; a program needn't handle non-finite values.
Results may differ from the reference program's by a relative error of at most 0.0033.
The reference program's roundings to bfloat16 on the way count: a program that leaves them out, or rounds other values in their place, can miss the bound.
Values may be sent and summed in bfloat16 or wider, within the bound.
No kernel may reach another device: no remote copies, remote signals or barrier semaphores. Data moves between devices by JAX's collectives and lax.ppermute only.
A program may use at most 128 MiB of HBM per device.

```python
import jax
import jax.numpy as jnp
from jax import lax

BLK = 128
STATES = 12
CX = 256
OB_DEV = 128
SEND_DEV = 768
TILES_DEV = 384
CAP = 192
NX = 1024
NY = 1024
OLD_BLOCKS = 4096
PAIRS = 24576
TILES = 12288
N_GX = 4
N_GY = 8
DEVICES = 32


def draw_dest_device(key, part):
    lowest = SEND_DEV - SEND_DEV // 4
    steps_x = jnp.array([-1, -1, -1, 0, 0, 1, 1, 1], jnp.int32)
    steps_y = jnp.array([-1, 0, 1, -1, 1, -1, 0, 1], jnp.int32)

    def one_device(device_key, device):
        first_key, second_key = jax.random.split(device_key)
        row_index = device // N_GY
        col_index = device % N_GY
        near_x = row_index + steps_x
        near_y = col_index + steps_y
        valid = (near_x >= 0) & (near_x < N_GX) & (near_y >= 0) & (near_y < N_GY)
        near = near_x * N_GY + near_y
        candidate = jnp.arange(8 * CAP, dtype=jnp.int32) // CAP
        scores = jax.random.permutation(first_key, 8 * CAP).astype(jnp.int32) + jnp.where(valid[candidate], 0, 8 * CAP).astype(jnp.int32)
        picked = candidate[jnp.argsort(scores)[:SEND_DEV - CAP]]
        others = near[picked]
        destination = jnp.concatenate([jnp.full((CAP,), device, jnp.int32), others.astype(jnp.int32)])
        shuffle = jax.random.permutation(second_key, lowest)
        leading = destination[:lowest][shuffle]
        return jnp.concatenate([leading, destination[lowest:]]).astype(jnp.int32)
    device_keys = jax.random.split(jax.random.fold_in(key, 11), DEVICES)
    return jax.vmap(one_device)(device_keys, jnp.arange(DEVICES, dtype=jnp.int32)).reshape(-1)


def draw_send_count(key, part):
    lowest = SEND_DEV - SEND_DEV // 4
    first_key, second_key = jax.random.split(jax.random.fold_in(key, 23))
    counts = jax.random.randint(first_key, (DEVICES,), lowest, SEND_DEV + 1)
    ordering = jax.random.permutation(second_key, DEVICES)
    counts = counts.at[ordering[0]].set(SEND_DEV).at[ordering[1]].set(lowest)
    return counts.astype(jnp.int32)


def set_ends(drawn, rng, low, largest):
    extent = drawn.shape
    spot = [jax.random.randint(jax.random.fold_in(rng, axis), (), 0, extent[axis]) for axis in range(len(extent))]
    drawn = drawn.at[tuple(spot)].set(low)
    longest = extent.index(max(extent))
    spot[longest] = (spot[longest] + 1) % extent[longest]
    return drawn.at[tuple(spot)].set(largest)


def block_scale(rng, dims, cuts, smallest, high):
    def one(position, shards_of):
        heights = jax.random.uniform(jax.random.fold_in(jax.random.fold_in(rng, 6), position), (shards_of,), jnp.float32, smallest / len(cuts), high / len(cuts))
        return jnp.repeat(jnp.exp(heights), dims[position] // shards_of).reshape((-1,) + (1,) * (len(dims) - position - 1))

    gain = one(*cuts[0])
    for cut in cuts[1:]:
        gain = gain * one(*cut)
    return gain


def noise(stream_key, shape, scale, reach, cuts=(), kind=jnp.bfloat16):
    entries = scale * jax.random.normal(stream_key, shape, jnp.float32)
    if cuts:
        entries = entries * block_scale(stream_key, shape, cuts, -0.22, 0.18)
    return jnp.clip(entries, -reach, reach).astype(kind)


def setup_inputs(seed: int = 0) -> dict:
    streams_of = jax.random.split(jax.random.key(seed), 9)
    old_states = noise(streams_of[0], (OLD_BLOCKS, STATES, BLK), 1.0, 6.0, ((0, 32),))
    weight_tiles = noise(streams_of[1], (TILES, BLK, BLK), BLK ** -0.5, 0.5, ((0, 32),))
    source_block = set_ends(jax.random.randint(streams_of[2], (PAIRS,), 0, OB_DEV), jax.random.fold_in(streams_of[2], 1), 0, OB_DEV - 1).astype(jnp.int32)
    tile_index = set_ends(jax.random.randint(streams_of[3], (PAIRS,), 0, TILES_DEV), jax.random.fold_in(streams_of[3], 1), 0, TILES_DEV - 1).astype(jnp.int32)
    dest_device = draw_dest_device(jax.random.fold_in(streams_of[8], 71), 0)
    dest_block = set_ends(jax.random.randint(streams_of[5], (PAIRS,), 0, CX), jax.random.fold_in(streams_of[5], 1), 0, CX - 1).astype(jnp.int32)
    send_count = draw_send_count(jax.random.fold_in(streams_of[8], 71), 0)
    velocity = noise(streams_of[7], (2, NX, NY), 1.0, 4.0, ((1, 4), (2, 8)), jnp.float32)
    return dict(old_states=old_states, weight_tiles=weight_tiles, source_block=source_block, tile_index=tile_index, dest_device=dest_device, dest_block=dest_block, send_count=send_count, velocity=velocity)


time_step = 0.2
shape_factor = 0.95
interaction = 0.01
shear_modulus = 1.0
fiber_number = 2.0

def product(left, right):
    return [[sum((left[first][inner] * right[inner][second] for inner in range(3))) for second in range(3)] for first in range(3)]

def advance(state_pad, flow_pad):
    centre = state_pad[1:-1, :, 1:-1]
    flow_x = flow_pad[0, 1:-1, 1:-1]
    flow_y = flow_pad[1, 1:-1, 1:-1]
    grad_xx = 0.5 * (flow_pad[0, 2:, 1:-1] - flow_pad[0, :-2, 1:-1])
    grad_xy = 0.5 * (flow_pad[0, 1:-1, 2:] - flow_pad[0, 1:-1, :-2])
    grad_yx = 0.5 * (flow_pad[1, 2:, 1:-1] - flow_pad[1, :-2, 1:-1])
    grad_yy = 0.5 * (flow_pad[1, 1:-1, 2:] - flow_pad[1, 1:-1, :-2])
    grad_zz = -(grad_xx + grad_yy)
    strain_xy = 0.5 * (grad_xy + grad_yx)
    spin_xy = 0.5 * (grad_xy - grad_yx)
    upwind = jnp.maximum(flow_x, 0.0)[:, None, :] * (centre - state_pad[:-2, :, 1:-1]) + jnp.minimum(flow_x, 0.0)[:, None, :] * (state_pad[2:, :, 1:-1] - centre) + jnp.maximum(flow_y, 0.0)[:, None, :] * (centre - state_pad[1:-1, :, :-2]) + jnp.minimum(flow_y, 0.0)[:, None, :] * (state_pad[1:-1, :, 2:] - centre)
    parts = [centre[:, index, :] for index in range(6)]
    orient = [[parts[0], parts[3], parts[4]], [parts[3], parts[1], parts[5]], [parts[4], parts[5], parts[2]]]
    zero = jnp.zeros_like(grad_xx)
    rate = [[grad_xx, strain_xy, zero], [strain_xy, grad_yy, zero], [zero, zero, grad_zz]]
    spin = [[zero, spin_xy, zero], [-spin_xy, zero, zero], [zero, zero, zero]]
    contraction = sum((orient[first][second] * rate[first][second] for first in range(3) for second in range(3)))
    shear = jnp.sqrt(2.0 * sum((rate[first][second] * rate[first][second] for first in range(3) for second in range(3))) + 1.0)
    spin_orient = product(spin, orient)
    orient_spin = product(orient, spin)
    rate_orient = product(rate, orient)
    orient_rate = product(orient, rate)
    sources = []
    for first, second in ((0, 0), (1, 1), (2, 2), (0, 1), (0, 2), (1, 2)):
        delta = 1.0 if first == second else 0.0
        sources.append(spin_orient[first][second] - orient_spin[first][second] + shape_factor * (rate_orient[first][second] + orient_rate[first][second] - 2.0 * contraction * orient[first][second]) + 2.0 * interaction * shear * (delta - 3.0 * orient[first][second]))
    sources = sources + [grad_xx, grad_yy, strain_xy]
    for first, second in ((0, 0), (1, 1), (0, 1)):
        sources.append(2.0 * shear_modulus * (rate[first][second] + fiber_number * contraction * orient[first][second]))
    source = jnp.stack(sources, axis=1)
    return centre + time_step * (source - upwind)

def reference(old_states, weight_tiles, source_block, tile_index, dest_device, dest_block, send_count, velocity):
    blocks_all = old_states.reshape(DEVICES, OB_DEV, STATES, BLK)
    tiles_all = weight_tiles.reshape(DEVICES, TILES_DEV, BLK, BLK)
    sources_all = source_block.reshape(DEVICES, SEND_DEV)
    picks_all = tile_index.reshape(DEVICES, SEND_DEV)
    targets_all = dest_device.reshape(DEVICES, SEND_DEV)
    rows_all = dest_block.reshape(DEVICES, SEND_DEV)

    def one_device(carry, items):
        blocks, tiles, source_ids, pick_ids, target_ids, row_ids, count = items
        block_pick = blocks[source_ids].astype(jnp.float32)
        tile_pick = tiles[pick_ids].astype(jnp.float32)
        pieces = jnp.einsum('snk,sck->scn', tile_pick, block_pick, precision=lax.Precision.HIGHEST)
        is_live = jnp.arange(SEND_DEV) < count
        pieces = jnp.where(is_live[:, None, None], pieces, 0.0)
        pieces = lax.optimization_barrier(pieces.astype(jnp.bfloat16)).astype(jnp.float32)
        tile_x = target_ids // N_GY
        tile_y = target_ids % N_GY
        carry = carry.at[tile_x, row_ids, tile_y].add(pieces)
        return (carry, None)
    start = jnp.zeros((N_GX, CX, N_GY, STATES, BLK), jnp.float32)
    total, _ = lax.scan(one_device, start, (blocks_all, tiles_all, sources_all, picks_all, targets_all, rows_all, send_count))
    remapped = total.transpose(0, 1, 3, 2, 4).reshape(NX, STATES, NY)
    state_pad = jnp.pad(remapped, ((1, 1), (0, 0), (1, 1)))
    flow_pad = jnp.pad(velocity, ((0, 0), (1, 1), (1, 1)))
    return advance(state_pad, flow_pad)
```

```python
import jax
import jax.numpy as jnp
from jax import lax
from jax.sharding import PartitionSpec as P

time_step = 0.2
shape_factor = 0.95
interaction = 0.01
shear_modulus = 1.0
fiber_number = 2.0


def shift_in(value, axis, step):
    count = lax.axis_size(axis)
    pairs = [(source, source + step) for source in range(count) if 0 <= source + step < count]
    return lax.ppermute(value, axis, pairs)


def neighbours(x, dim_x, dim_y):
    length_x = x.shape[dim_x]
    length_y = x.shape[dim_y]
    last_x = lax.slice_in_dim(x, length_x - 1, length_x, axis=dim_x)
    first_x = lax.slice_in_dim(x, 0, 1, axis=dim_x)
    before_x = shift_in(last_x, "gx", 1)
    after_x = shift_in(first_x, "gx", -1)
    prev_x = jnp.concatenate([before_x, lax.slice_in_dim(x, 0, length_x - 1, axis=dim_x)], axis=dim_x)
    next_x = jnp.concatenate([lax.slice_in_dim(x, 1, length_x, axis=dim_x), after_x], axis=dim_x)
    last_y = jnp.moveaxis(lax.index_in_dim(x, length_y - 1, axis=dim_y, keepdims=False), dim_x, -1)
    first_y = jnp.moveaxis(lax.index_in_dim(x, 0, axis=dim_y, keepdims=False), dim_x, -1)
    before_y = jnp.expand_dims(jnp.moveaxis(shift_in(last_y, "gy", 1), -1, dim_x), dim_y)
    after_y = jnp.expand_dims(jnp.moveaxis(shift_in(first_y, "gy", -1), -1, dim_x), dim_y)
    prev_y = jnp.concatenate([before_y, lax.slice_in_dim(x, 0, length_y - 1, axis=dim_y)], axis=dim_y)
    next_y = jnp.concatenate([lax.slice_in_dim(x, 1, length_y, axis=dim_y), after_y], axis=dim_y)
    return prev_x, next_x, prev_y, next_y


def product(left, right):
    return [
        [
            sum((left[first][inner] * right[inner][second] for inner in range(3)))
            for second in range(3)
        ]
        for first in range(3)
    ]


def advance(centre, state_near, flow, flow_near):
    prev_x, next_x, prev_y, next_y = state_near
    vprev_x, vnext_x, vprev_y, vnext_y = flow_near
    flow_x = flow[0]
    flow_y = flow[1]
    grad_xx = 0.5 * (vnext_x[0] - vprev_x[0])
    grad_xy = 0.5 * (vnext_y[0] - vprev_y[0])
    grad_yx = 0.5 * (vnext_x[1] - vprev_x[1])
    grad_yy = 0.5 * (vnext_y[1] - vprev_y[1])
    grad_zz = -(grad_xx + grad_yy)
    strain_xy = 0.5 * (grad_xy + grad_yx)
    spin_xy = 0.5 * (grad_xy - grad_yx)
    upwind = (
        jnp.maximum(flow_x, 0.0)[:, None, :] * (centre - prev_x)
        + jnp.minimum(flow_x, 0.0)[:, None, :] * (next_x - centre)
        + jnp.maximum(flow_y, 0.0)[:, None, :] * (centre - prev_y)
        + jnp.minimum(flow_y, 0.0)[:, None, :] * (next_y - centre)
    )
    parts = [centre[:, index, :] for index in range(6)]
    orient = [
        [parts[0], parts[3], parts[4]],
        [parts[3], parts[1], parts[5]],
        [parts[4], parts[5], parts[2]],
    ]
    zero = jnp.zeros_like(grad_xx)
    rate = [[grad_xx, strain_xy, zero], [strain_xy, grad_yy, zero], [zero, zero, grad_zz]]
    spin = [[zero, spin_xy, zero], [-spin_xy, zero, zero], [zero, zero, zero]]
    contraction = sum(
        (orient[first][second] * rate[first][second] for first in range(3) for second in range(3))
    )
    shear = jnp.sqrt(
        2.0
        * sum(
            (rate[first][second] * rate[first][second] for first in range(3) for second in range(3))
        )
        + 1.0
    )
    spin_orient = product(spin, orient)
    orient_spin = product(orient, spin)
    rate_orient = product(rate, orient)
    orient_rate = product(orient, rate)
    sources = []
    for first, second in ((0, 0), (1, 1), (2, 2), (0, 1), (0, 2), (1, 2)):
        delta = 1.0 if first == second else 0.0
        sources.append(
            spin_orient[first][second]
            - orient_spin[first][second]
            + shape_factor
            * (
                rate_orient[first][second]
                + orient_rate[first][second]
                - 2.0 * contraction * orient[first][second]
            )
            + 2.0 * interaction * shear * (delta - 3.0 * orient[first][second])
        )
    sources = sources + [grad_xx, grad_yy, strain_xy]
    for first, second in ((0, 0), (1, 1), (0, 1)):
        sources.append(
            2.0
            * shear_modulus
            * (rate[first][second] + fiber_number * contraction * orient[first][second])
        )
    source = jnp.stack(sources, axis=1)
    return centre + time_step * (source - upwind)


def per_device(
    old_states,
    weight_tiles,
    source_block,
    tile_index,
    dest_device,
    dest_block,
    send_count,
    velocity,
):
    flow_near = neighbours(velocity, 1, 2)
    slot_count = source_block.shape[0]
    block_count = old_states.shape[0]
    state_count = old_states.shape[1]
    lane_count = old_states.shape[2]
    tile_rows = velocity.shape[1]
    block_onehot = (source_block[:, None] == jnp.arange(block_count)[None, :]).astype(jnp.bfloat16)
    block_pick = jnp.dot(
        block_onehot,
        old_states.reshape(block_count, state_count * lane_count),
        preferred_element_type=jnp.float32,
    )
    block_pick = block_pick.astype(jnp.bfloat16).reshape(slot_count, state_count, lane_count)
    tile_pick = weight_tiles[tile_index]
    pieces = jnp.einsum("snk,sck->scn", tile_pick, block_pick, preferred_element_type=jnp.float32)
    is_live = jnp.arange(slot_count) < send_count[0]
    pieces = jnp.where(is_live[:, None, None], pieces, 0.0).astype(jnp.bfloat16)
    tags = jnp.broadcast_to(dest_block.astype(jnp.bfloat16)[:, None, None], (slot_count, 1, lane_count))
    pieces = jnp.concatenate([pieces, tags], axis=1)
    channels = state_count + 1
    width_y = lax.axis_size("gy")
    width_x = lax.axis_size("gx")
    capacity = slot_count // 4
    own_x = lax.axis_index("gx")
    own_y = lax.axis_index("gy")
    step_x = dest_device // width_y - own_x
    step_y = dest_device % width_y - own_y
    direction = (step_x + 1) * 3 + (step_y + 1)
    matches = ((direction[:, None] == jnp.arange(9)[None, :]) & is_live[:, None]).astype(jnp.int32)
    earlier = jnp.cumsum(matches, axis=0) - matches
    position = jnp.sum(earlier * matches, axis=1)
    target = jnp.where(is_live, direction * capacity + position, 9 * capacity)
    placing = target[None, :] == jnp.arange(9 * capacity)[:, None]
    outgoing = jnp.dot(
        placing.astype(jnp.bfloat16),
        pieces.reshape(slot_count, channels * lane_count),
        preferred_element_type=jnp.float32,
    )
    outgoing = outgoing.astype(jnp.bfloat16).reshape(3, 3, capacity, channels, lane_count)
    received = [outgoing[1, 1]]
    for move_x in (-1, 0, 1):
        for move_y in (-1, 0, 1):
            if move_x != 0 or move_y != 0:
                pairs = []
                for source_x in range(width_x):
                    for source_y in range(width_y):
                        goal_x = source_x + move_x
                        goal_y = source_y + move_y
                        if 0 <= goal_x < width_x and 0 <= goal_y < width_y:
                            pairs.append((source_x * width_y + source_y, goal_x * width_y + goal_y))
                received.append(lax.ppermute(outgoing[move_x + 1, move_y + 1], ("gx", "gy"), pairs))
    arrived = jnp.concatenate(received, axis=0)
    arrived_rows = arrived[:, :state_count, :].reshape(-1, state_count * lane_count)
    arrived_ids = arrived[:, state_count, 0].astype(jnp.int32)
    selector = (jnp.arange(tile_rows)[:, None] == arrived_ids[None, :]).astype(jnp.bfloat16)
    remapped = jnp.dot(selector, arrived_rows, preferred_element_type=jnp.float32).reshape(
        tile_rows, state_count, lane_count
    )
    state_near = neighbours(remapped, 0, 2)
    return advance(remapped, state_near, velocity, flow_near)


def solution(mesh):
    in_specs = (
        P(("gx", "gy"), None, None),
        P(("gx", "gy"), None, None),
        P(("gx", "gy")),
        P(("gx", "gy")),
        P(("gx", "gy")),
        P(("gx", "gy")),
        P(("gx", "gy")),
        P(None, "gx", "gy"),
    )
    out_specs = P("gx", None, "gy")
    return jax.shard_map(
        per_device, mesh=mesh, in_specs=in_specs, out_specs=out_specs, check_vma=False
    )
```

```python
import jax
import jax.numpy as jnp
from jax import lax
from jax.sharding import PartitionSpec as P
from jax.experimental import pallas as pl
from jax.experimental.pallas import tpu as pltpu

time_step = 0.2
shape_factor = 0.95
interaction = 0.01
shear_modulus = 1.0
fiber_number = 2.0


GROUP = 32


def contribution_kernel(tile_ref, source_ref, count_ref, old_ref, weight_hbm, out_ref, weight_buf, sems):
    step = pl.program_id(0)
    steps = pl.num_programs(0)

    def fetch(chunk, slot):
        for member in range(GROUP):
            tile = tile_ref[chunk * GROUP + member]
            pltpu.make_async_copy(
                weight_hbm.at[tile], weight_buf.at[slot, member], sems.at[slot, member]
            ).start()

    @pl.when(step == 0)
    def _():
        fetch(0, 0)

    @pl.when(step + 1 < steps)
    def _():
        fetch(step + 1, (step + 1) % 2)

    slot = step % 2
    for member in range(GROUP):
        pltpu.make_async_copy(
            weight_hbm.at[0], weight_buf.at[slot, member], sems.at[slot, member]
        ).wait()
    count = count_ref[0]
    for member in range(GROUP):
        index = step * GROUP + member
        block = old_ref[source_ref[index]]
        weight = weight_buf[slot, member]
        piece = lax.dot_general(
            block, weight, (((1,), (1,)), ((), ())), preferred_element_type=jnp.float32
        )
        piece = jnp.where(index < count, piece, 0.0)
        out_ref[member] = piece.astype(out_ref.dtype)


def contributions(old_states, weight_tiles, source_block, tile_index, send_count):
    slot_count = source_block.shape[0]
    block_count, state_count, lane_count = old_states.shape
    rows = weight_tiles.shape[1]
    grid_spec = pltpu.PrefetchScalarGridSpec(
        num_scalar_prefetch=3,
        grid=(slot_count // GROUP,),
        in_specs=[
            pl.BlockSpec((block_count, state_count, lane_count), lambda i, *_: (0, 0, 0)),
            pl.BlockSpec(memory_space=pl.ANY),
        ],
        out_specs=pl.BlockSpec((GROUP, state_count, rows), lambda i, *_: (i, 0, 0)),
        scratch_shapes=[
            pltpu.VMEM((2, GROUP) + weight_tiles.shape[1:], weight_tiles.dtype),
            pltpu.SemaphoreType.DMA((2, GROUP)),
        ],
    )
    return pl.pallas_call(
        contribution_kernel,
        grid_spec=grid_spec,
        out_shape=jax.ShapeDtypeStruct((slot_count, state_count, rows), jnp.bfloat16),
        compiler_params=pltpu.CompilerParams(dimension_semantics=("arbitrary",)),
    )(tile_index, source_block, send_count, old_states, weight_tiles)


def shift_in(value, axis, step):
    count = lax.axis_size(axis)
    pairs = [(source, source + step) for source in range(count) if 0 <= source + step < count]
    return lax.ppermute(value, axis, pairs)


def neighbours(x, dim_x, dim_y):
    length_x = x.shape[dim_x]
    length_y = x.shape[dim_y]
    last_x = lax.slice_in_dim(x, length_x - 1, length_x, axis=dim_x)
    first_x = lax.slice_in_dim(x, 0, 1, axis=dim_x)
    before_x = shift_in(last_x, "gx", 1)
    after_x = shift_in(first_x, "gx", -1)
    prev_x = jnp.concatenate([before_x, lax.slice_in_dim(x, 0, length_x - 1, axis=dim_x)], axis=dim_x)
    next_x = jnp.concatenate([lax.slice_in_dim(x, 1, length_x, axis=dim_x), after_x], axis=dim_x)
    last_y = jnp.moveaxis(lax.index_in_dim(x, length_y - 1, axis=dim_y, keepdims=False), dim_x, -1)
    first_y = jnp.moveaxis(lax.index_in_dim(x, 0, axis=dim_y, keepdims=False), dim_x, -1)
    before_y = jnp.expand_dims(jnp.moveaxis(shift_in(last_y, "gy", 1), -1, dim_x), dim_y)
    after_y = jnp.expand_dims(jnp.moveaxis(shift_in(first_y, "gy", -1), -1, dim_x), dim_y)
    prev_y = jnp.concatenate([before_y, lax.slice_in_dim(x, 0, length_y - 1, axis=dim_y)], axis=dim_y)
    next_y = jnp.concatenate([lax.slice_in_dim(x, 1, length_y, axis=dim_y), after_y], axis=dim_y)
    return prev_x, next_x, prev_y, next_y


def product(left, right):
    return [
        [
            sum((left[first][inner] * right[inner][second] for inner in range(3)))
            for second in range(3)
        ]
        for first in range(3)
    ]


def advance(centre, state_near, flow, flow_near):
    prev_x, next_x, prev_y, next_y = state_near
    vprev_x, vnext_x, vprev_y, vnext_y = flow_near
    flow_x = flow[0]
    flow_y = flow[1]
    grad_xx = 0.5 * (vnext_x[0] - vprev_x[0])
    grad_xy = 0.5 * (vnext_y[0] - vprev_y[0])
    grad_yx = 0.5 * (vnext_x[1] - vprev_x[1])
    grad_yy = 0.5 * (vnext_y[1] - vprev_y[1])
    grad_zz = -(grad_xx + grad_yy)
    strain_xy = 0.5 * (grad_xy + grad_yx)
    spin_xy = 0.5 * (grad_xy - grad_yx)
    upwind = (
        jnp.maximum(flow_x, 0.0)[:, None, :] * (centre - prev_x)
        + jnp.minimum(flow_x, 0.0)[:, None, :] * (next_x - centre)
        + jnp.maximum(flow_y, 0.0)[:, None, :] * (centre - prev_y)
        + jnp.minimum(flow_y, 0.0)[:, None, :] * (next_y - centre)
    )
    parts = [centre[:, index, :] for index in range(6)]
    orient = [
        [parts[0], parts[3], parts[4]],
        [parts[3], parts[1], parts[5]],
        [parts[4], parts[5], parts[2]],
    ]
    zero = jnp.zeros_like(grad_xx)
    rate = [[grad_xx, strain_xy, zero], [strain_xy, grad_yy, zero], [zero, zero, grad_zz]]
    spin = [[zero, spin_xy, zero], [-spin_xy, zero, zero], [zero, zero, zero]]
    contraction = sum(
        (orient[first][second] * rate[first][second] for first in range(3) for second in range(3))
    )
    shear = jnp.sqrt(
        2.0
        * sum(
            (rate[first][second] * rate[first][second] for first in range(3) for second in range(3))
        )
        + 1.0
    )
    spin_orient = product(spin, orient)
    orient_spin = product(orient, spin)
    rate_orient = product(rate, orient)
    orient_rate = product(orient, rate)
    sources = []
    for first, second in ((0, 0), (1, 1), (2, 2), (0, 1), (0, 2), (1, 2)):
        delta = 1.0 if first == second else 0.0
        sources.append(
            spin_orient[first][second]
            - orient_spin[first][second]
            + shape_factor
            * (
                rate_orient[first][second]
                + orient_rate[first][second]
                - 2.0 * contraction * orient[first][second]
            )
            + 2.0 * interaction * shear * (delta - 3.0 * orient[first][second])
        )
    sources = sources + [grad_xx, grad_yy, strain_xy]
    for first, second in ((0, 0), (1, 1), (0, 1)):
        sources.append(
            2.0
            * shear_modulus
            * (rate[first][second] + fiber_number * contraction * orient[first][second])
        )
    source = jnp.stack(sources, axis=1)
    return centre + time_step * (source - upwind)


def per_device(
    old_states,
    weight_tiles,
    source_block,
    tile_index,
    dest_device,
    dest_block,
    send_count,
    velocity,
):
    flow_near = neighbours(velocity, 1, 2)
    slot_count = source_block.shape[0]
    block_count = old_states.shape[0]
    state_count = old_states.shape[1]
    lane_count = old_states.shape[2]
    tile_rows = velocity.shape[1]
    pieces = contributions(old_states, weight_tiles, source_block, tile_index, send_count)
    is_live = jnp.arange(slot_count) < send_count[0]
    width_y = lax.axis_size("gy")
    width_x = lax.axis_size("gx")
    capacity = slot_count // 4
    own_x = lax.axis_index("gx")
    own_y = lax.axis_index("gy")
    step_x = dest_device // width_y - own_x
    step_y = dest_device % width_y - own_y
    direction = (step_x + 1) * 3 + (step_y + 1)
    matches = ((direction[:, None] == jnp.arange(9)[None, :]) & is_live[:, None]).astype(jnp.int32)
    earlier = jnp.cumsum(matches, axis=0) - matches
    position = jnp.sum(earlier * matches, axis=1)
    target = jnp.where(is_live, direction * capacity + position, 9 * capacity)
    placing = target[None, :] == jnp.arange(9 * capacity)[:, None]
    outgoing = jnp.einsum(
        "ps,scn->cpn", placing.astype(jnp.bfloat16), pieces, preferred_element_type=jnp.float32
    ).astype(jnp.bfloat16)
    labels = jnp.sum(jnp.where(placing, dest_block[None, :], 0), axis=1).astype(jnp.bfloat16)
    tags = jnp.broadcast_to(labels[None, :, None], (1, 9 * capacity, lane_count))
    outgoing = jnp.concatenate([outgoing, tags], axis=0)
    channels = state_count + 1
    remapped = None
    for move_x in (-1, 0, 1):
        for move_y in (-1, 0, 1):
            begin = ((move_x + 1) * 3 + (move_y + 1)) * capacity
            chunk = outgoing[:, begin:begin + capacity, :]
            if move_x != 0 or move_y != 0:
                pairs = []
                for source_x in range(width_x):
                    for source_y in range(width_y):
                        goal_x = source_x + move_x
                        goal_y = source_y + move_y
                        if 0 <= goal_x < width_x and 0 <= goal_y < width_y:
                            pairs.append((source_x * width_y + source_y, goal_x * width_y + goal_y))
                chunk = lax.ppermute(chunk, ("gx", "gy"), pairs)
            ids = chunk[state_count, :, 0].astype(jnp.int32)
            selector = (jnp.arange(tile_rows)[:, None] == ids[None, :]).astype(jnp.bfloat16)
            part = jnp.einsum(
                "rp,cpn->rcn", selector, chunk[:state_count], preferred_element_type=jnp.float32
            )
            remapped = part if remapped is None else remapped + part
    state_near = neighbours(remapped, 0, 2)
    return advance(remapped, state_near, velocity, flow_near)


def solution(mesh):
    in_specs = (
        P(("gx", "gy"), None, None),
        P(("gx", "gy"), None, None),
        P(("gx", "gy")),
        P(("gx", "gy")),
        P(("gx", "gy")),
        P(("gx", "gy")),
        P(("gx", "gy")),
        P(None, "gx", "gy"),
    )
    out_specs = P("gx", None, "gy")
    return jax.shard_map(
        per_device, mesh=mesh, in_specs=in_specs, out_specs=out_specs, check_vma=False
    )
```

```python
import jax
import jax.numpy as jnp
from jax import lax
from jax.sharding import PartitionSpec as P
from jax.experimental import pallas as pl
from jax.experimental.pallas import tpu as pltpu

time_step = 0.2
shape_factor = 0.95
interaction = 0.01
shear_modulus = 1.0
fiber_number = 2.0


GROUP = 64


def contribution_kernel(tile_ref, source_ref, count_ref, label_ref, old_ref, weight_hbm, out_ref, weight_buf, sems):
    step = pl.program_id(0)
    steps = pl.num_programs(0)

    def fetch(chunk, slot):
        for member in range(GROUP):
            tile = tile_ref[chunk * GROUP + member]
            pltpu.make_async_copy(
                weight_hbm.at[tile], weight_buf.at[slot, member], sems.at[slot, member]
            ).start()

    @pl.when(step == 0)
    def _():
        fetch(0, 0)

    @pl.when(step + 1 < steps)
    def _():
        fetch(step + 1, (step + 1) % 2)

    slot = step % 2
    for member in range(GROUP):
        pltpu.make_async_copy(
            weight_hbm.at[0], weight_buf.at[slot, member], sems.at[slot, member]
        ).wait()
    count = count_ref[0]
    for member in range(GROUP):
        index = step * GROUP + member
        block = old_ref[source_ref[index]]
        weight = weight_buf[slot, member]
        piece = lax.dot_general(
            block, weight, (((1,), (1,)), ((), ())), preferred_element_type=jnp.float32
        )
        piece = jnp.where(index < count, piece, 0.0)
        states = piece.shape[0]
        out_ref[member, pl.ds(0, states), :] = piece.astype(out_ref.dtype)
        tag = jnp.full((1, piece.shape[1]), label_ref[index].astype(jnp.float32), jnp.float32)
        out_ref[member, pl.ds(states, 1), :] = tag.astype(out_ref.dtype)


def contributions(old_states, weight_tiles, source_block, tile_index, send_count, dest_block):
    slot_count = source_block.shape[0]
    block_count, state_count, lane_count = old_states.shape
    rows = weight_tiles.shape[1]
    grid_spec = pltpu.PrefetchScalarGridSpec(
        num_scalar_prefetch=4,
        grid=(slot_count // GROUP,),
        in_specs=[
            pl.BlockSpec((block_count, state_count, lane_count), lambda i, *_: (0, 0, 0)),
            pl.BlockSpec(memory_space=pl.ANY),
        ],
        out_specs=pl.BlockSpec((GROUP, state_count + 1, rows), lambda i, *_: (i, 0, 0)),
        scratch_shapes=[
            pltpu.VMEM((2, GROUP) + weight_tiles.shape[1:], weight_tiles.dtype),
            pltpu.SemaphoreType.DMA((2, GROUP)),
        ],
    )
    return pl.pallas_call(
        contribution_kernel,
        grid_spec=grid_spec,
        out_shape=jax.ShapeDtypeStruct((slot_count, state_count + 1, rows), jnp.bfloat16),
        compiler_params=pltpu.CompilerParams(dimension_semantics=("arbitrary",)),
    )(tile_index, source_block, send_count, dest_block, old_states, weight_tiles)


def shift_in(value, axis, step):
    count = lax.axis_size(axis)
    pairs = [(source, source + step) for source in range(count) if 0 <= source + step < count]
    return lax.ppermute(value, axis, pairs)


def neighbours(x, dim_x, dim_y):
    length_x = x.shape[dim_x]
    length_y = x.shape[dim_y]
    last_x = lax.slice_in_dim(x, length_x - 1, length_x, axis=dim_x)
    first_x = lax.slice_in_dim(x, 0, 1, axis=dim_x)
    last_y = jnp.moveaxis(lax.index_in_dim(x, length_y - 1, axis=dim_y, keepdims=False), dim_x, -1)
    first_y = jnp.moveaxis(lax.index_in_dim(x, 0, axis=dim_y, keepdims=False), dim_x, -1)
    return assemble(x, dim_x, dim_y, first_x, last_x, first_y, last_y)


def assemble(x, dim_x, dim_y, first_x, last_x, first_y, last_y):
    length_x = x.shape[dim_x]
    length_y = x.shape[dim_y]
    before_x = shift_in(last_x, "gx", 1)
    after_x = shift_in(first_x, "gx", -1)
    before_y = jnp.expand_dims(jnp.moveaxis(shift_in(last_y, "gy", 1), -1, dim_x), dim_y)
    after_y = jnp.expand_dims(jnp.moveaxis(shift_in(first_y, "gy", -1), -1, dim_x), dim_y)
    prev_x = jnp.concatenate([before_x, lax.slice_in_dim(x, 0, length_x - 1, axis=dim_x)], axis=dim_x)
    next_x = jnp.concatenate([lax.slice_in_dim(x, 1, length_x, axis=dim_x), after_x], axis=dim_x)
    prev_y = jnp.concatenate([before_y, lax.slice_in_dim(x, 0, length_y - 1, axis=dim_y)], axis=dim_y)
    next_y = jnp.concatenate([lax.slice_in_dim(x, 1, length_y, axis=dim_y), after_y], axis=dim_y)
    return prev_x, next_x, prev_y, next_y


def product(left, right):
    return [
        [
            sum((left[first][inner] * right[inner][second] for inner in range(3)))
            for second in range(3)
        ]
        for first in range(3)
    ]


def advance(centre, state_near, flow, flow_near):
    prev_x, next_x, prev_y, next_y = state_near
    vprev_x, vnext_x, vprev_y, vnext_y = flow_near
    flow_x = flow[0]
    flow_y = flow[1]
    grad_xx = 0.5 * (vnext_x[0] - vprev_x[0])
    grad_xy = 0.5 * (vnext_y[0] - vprev_y[0])
    grad_yx = 0.5 * (vnext_x[1] - vprev_x[1])
    grad_yy = 0.5 * (vnext_y[1] - vprev_y[1])
    grad_zz = -(grad_xx + grad_yy)
    strain_xy = 0.5 * (grad_xy + grad_yx)
    spin_xy = 0.5 * (grad_xy - grad_yx)
    upwind = (
        jnp.maximum(flow_x, 0.0)[:, None, :] * (centre - prev_x)
        + jnp.minimum(flow_x, 0.0)[:, None, :] * (next_x - centre)
        + jnp.maximum(flow_y, 0.0)[:, None, :] * (centre - prev_y)
        + jnp.minimum(flow_y, 0.0)[:, None, :] * (next_y - centre)
    )
    parts = [centre[:, index, :] for index in range(6)]
    orient = [
        [parts[0], parts[3], parts[4]],
        [parts[3], parts[1], parts[5]],
        [parts[4], parts[5], parts[2]],
    ]
    zero = jnp.zeros_like(grad_xx)
    rate = [[grad_xx, strain_xy, zero], [strain_xy, grad_yy, zero], [zero, zero, grad_zz]]
    spin = [[zero, spin_xy, zero], [-spin_xy, zero, zero], [zero, zero, zero]]
    contraction = sum(
        (orient[first][second] * rate[first][second] for first in range(3) for second in range(3))
    )
    shear = jnp.sqrt(
        2.0
        * sum(
            (rate[first][second] * rate[first][second] for first in range(3) for second in range(3))
        )
        + 1.0
    )
    spin_orient = product(spin, orient)
    orient_spin = product(orient, spin)
    rate_orient = product(rate, orient)
    orient_rate = product(orient, rate)
    sources = []
    for first, second in ((0, 0), (1, 1), (2, 2), (0, 1), (0, 2), (1, 2)):
        delta = 1.0 if first == second else 0.0
        sources.append(
            spin_orient[first][second]
            - orient_spin[first][second]
            + shape_factor
            * (
                rate_orient[first][second]
                + orient_rate[first][second]
                - 2.0 * contraction * orient[first][second]
            )
            + 2.0 * interaction * shear * (delta - 3.0 * orient[first][second])
        )
    sources = sources + [grad_xx, grad_yy, strain_xy]
    for first, second in ((0, 0), (1, 1), (0, 1)):
        sources.append(
            2.0
            * shear_modulus
            * (rate[first][second] + fiber_number * contraction * orient[first][second])
        )
    source = jnp.stack(sources, axis=1)
    return centre + time_step * (source - upwind)


def per_device(
    old_states,
    weight_tiles,
    source_block,
    tile_index,
    dest_device,
    dest_block,
    send_count,
    velocity,
):
    flow_near = neighbours(velocity, 1, 2)
    slot_count = source_block.shape[0]
    block_count = old_states.shape[0]
    state_count = old_states.shape[1]
    lane_count = old_states.shape[2]
    tile_rows = velocity.shape[1]
    pieces = contributions(old_states, weight_tiles, source_block, tile_index, send_count, dest_block)
    is_live = jnp.arange(slot_count) < send_count[0]
    width_y = lax.axis_size("gy")
    width_x = lax.axis_size("gx")
    capacity = slot_count // 4
    own_x = lax.axis_index("gx")
    own_y = lax.axis_index("gy")
    step_x = dest_device // width_y - own_x
    step_y = dest_device % width_y - own_y
    direction = (step_x + 1) * 3 + (step_y + 1)
    matches = ((direction[:, None] == jnp.arange(9)[None, :]) & is_live[:, None]).astype(jnp.int32)
    earlier = jnp.cumsum(matches, axis=0) - matches
    position = jnp.sum(earlier * matches, axis=1)
    target = jnp.where(is_live, direction * capacity + position, 9 * capacity)
    placing = target[None, :] == jnp.arange(9 * capacity)[:, None]
    outgoing = jnp.einsum(
        "ps,scn->cpn", placing.astype(jnp.bfloat16), pieces, preferred_element_type=jnp.float32
    ).astype(jnp.bfloat16)
    channels = state_count + 1
    arrived = []
    for move_x in (-1, 0, 1):
        for move_y in (-1, 0, 1):
            begin = ((move_x + 1) * 3 + (move_y + 1)) * capacity
            chunk = outgoing[:, begin:begin + capacity, :]
            if move_x != 0 or move_y != 0:
                pairs = []
                for source_x in range(width_x):
                    for source_y in range(width_y):
                        goal_x = source_x + move_x
                        goal_y = source_y + move_y
                        if 0 <= goal_x < width_x and 0 <= goal_y < width_y:
                            pairs.append((source_x * width_y + source_y, goal_x * width_y + goal_y))
                chunk = lax.ppermute(chunk, ("gx", "gy"), pairs)
            ids = chunk[state_count, :, 0].astype(jnp.int32)
            selector = (jnp.arange(tile_rows)[:, None] == ids[None, :]).astype(jnp.bfloat16)
            arrived.append((selector, chunk[:state_count]))

    def gathered(pick_rows, pick_lanes):
        total = None
        for selector, data in arrived:
            part = jnp.einsum(
                "rp,cpn->rcn",
                pick_rows(selector),
                pick_lanes(data),
                preferred_element_type=jnp.float32,
            )
            total = part if total is None else total + part
        return total

    edge_rows = gathered(lambda sel: sel[jnp.array([0, tile_rows - 1])], lambda data: data)
    edge_cols = gathered(lambda sel: sel, lambda data: data[:, :, jnp.array([0, lane_count - 1])])
    remapped = gathered(lambda sel: sel, lambda data: data)
    state_near = assemble(
        remapped,
        0,
        2,
        edge_rows[0:1],
        edge_rows[1:2],
        edge_cols[:, :, 0].T,
        edge_cols[:, :, 1].T,
    )
    return advance(remapped, state_near, velocity, flow_near)


def solution(mesh):
    in_specs = (
        P(("gx", "gy"), None, None),
        P(("gx", "gy"), None, None),
        P(("gx", "gy")),
        P(("gx", "gy")),
        P(("gx", "gy")),
        P(("gx", "gy")),
        P(("gx", "gy")),
        P(None, "gx", "gy"),
    )
    out_specs = P("gx", None, "gy")
    return jax.shard_map(
        per_device, mesh=mesh, in_specs=in_specs, out_specs=out_specs, check_vma=False
    )
```

```python
import jax
import jax.numpy as jnp
from jax import lax
from jax.sharding import PartitionSpec as P
from jax.experimental import pallas as pl
from jax.experimental.pallas import tpu as pltpu

time_step = 0.2
shape_factor = 0.95
interaction = 0.01
shear_modulus = 1.0
fiber_number = 2.0


GROUP = 64


def contribution_kernel(tile_ref, source_ref, count_ref, label_ref, old_ref, weight_hbm, out_ref, weight_buf, sems):
    step = pl.program_id(0)
    steps = pl.num_programs(0)

    def fetch(chunk, slot):
        for member in range(GROUP):
            tile = tile_ref[chunk * GROUP + member]
            pltpu.make_async_copy(
                weight_hbm.at[tile], weight_buf.at[slot, member], sems.at[slot, member]
            ).start()

    @pl.when(step == 0)
    def _():
        fetch(0, 0)

    @pl.when(step + 1 < steps)
    def _():
        fetch(step + 1, (step + 1) % 2)

    slot = step % 2
    for member in range(GROUP):
        pltpu.make_async_copy(
            weight_hbm.at[0], weight_buf.at[slot, member], sems.at[slot, member]
        ).wait()
    count = count_ref[0]
    for member in range(GROUP):
        index = step * GROUP + member
        block = old_ref[source_ref[index]]
        weight = weight_buf[slot, member]
        piece = lax.dot_general(
            block, weight, (((1,), (1,)), ((), ())), preferred_element_type=jnp.float32
        )
        piece = jnp.where(index < count, piece, 0.0)
        states = piece.shape[0]
        out_ref[member, pl.ds(0, states), :] = piece.astype(out_ref.dtype)
        tag = jnp.full((1, piece.shape[1]), label_ref[index].astype(jnp.float32), jnp.float32)
        out_ref[member, pl.ds(states, 1), :] = tag.astype(out_ref.dtype)


def contributions(old_states, weight_tiles, source_block, tile_index, send_count, dest_block):
    slot_count = source_block.shape[0]
    block_count, state_count, lane_count = old_states.shape
    rows = weight_tiles.shape[1]
    grid_spec = pltpu.PrefetchScalarGridSpec(
        num_scalar_prefetch=4,
        grid=(slot_count // GROUP,),
        in_specs=[
            pl.BlockSpec((block_count, state_count, lane_count), lambda i, *_: (0, 0, 0)),
            pl.BlockSpec(memory_space=pl.ANY),
        ],
        out_specs=pl.BlockSpec((GROUP, state_count + 1, rows), lambda i, *_: (i, 0, 0)),
        scratch_shapes=[
            pltpu.VMEM((2, GROUP) + weight_tiles.shape[1:], weight_tiles.dtype),
            pltpu.SemaphoreType.DMA((2, GROUP)),
        ],
    )
    return pl.pallas_call(
        contribution_kernel,
        grid_spec=grid_spec,
        out_shape=jax.ShapeDtypeStruct((slot_count, state_count + 1, rows), jnp.bfloat16),
        compiler_params=pltpu.CompilerParams(dimension_semantics=("arbitrary",)),
    )(tile_index, source_block, send_count, dest_block, old_states, weight_tiles)


def shift_in(value, axis, step):
    count = lax.axis_size(axis)
    pairs = [(source, source + step) for source in range(count) if 0 <= source + step < count]
    return lax.ppermute(value, axis, pairs)


def neighbours(x, dim_x, dim_y):
    length_x = x.shape[dim_x]
    length_y = x.shape[dim_y]
    last_x = lax.slice_in_dim(x, length_x - 1, length_x, axis=dim_x)
    first_x = lax.slice_in_dim(x, 0, 1, axis=dim_x)
    last_y = jnp.moveaxis(lax.index_in_dim(x, length_y - 1, axis=dim_y, keepdims=False), dim_x, -1)
    first_y = jnp.moveaxis(lax.index_in_dim(x, 0, axis=dim_y, keepdims=False), dim_x, -1)
    return assemble(x, dim_x, dim_y, first_x, last_x, first_y, last_y)


def assemble(x, dim_x, dim_y, first_x, last_x, first_y, last_y):
    length_x = x.shape[dim_x]
    length_y = x.shape[dim_y]
    before_x = shift_in(last_x, "gx", 1)
    after_x = shift_in(first_x, "gx", -1)
    before_y = jnp.expand_dims(jnp.moveaxis(shift_in(last_y, "gy", 1), -1, dim_x), dim_y)
    after_y = jnp.expand_dims(jnp.moveaxis(shift_in(first_y, "gy", -1), -1, dim_x), dim_y)
    prev_x = jnp.concatenate([before_x, lax.slice_in_dim(x, 0, length_x - 1, axis=dim_x)], axis=dim_x)
    next_x = jnp.concatenate([lax.slice_in_dim(x, 1, length_x, axis=dim_x), after_x], axis=dim_x)
    prev_y = jnp.concatenate([before_y, lax.slice_in_dim(x, 0, length_y - 1, axis=dim_y)], axis=dim_y)
    next_y = jnp.concatenate([lax.slice_in_dim(x, 1, length_y, axis=dim_y), after_y], axis=dim_y)
    return prev_x, next_x, prev_y, next_y


def product(left, right):
    return [
        [
            sum((left[first][inner] * right[inner][second] for inner in range(3)))
            for second in range(3)
        ]
        for first in range(3)
    ]


def advance(centre, state_near, flow, flow_near):
    prev_x, next_x, prev_y, next_y = state_near
    vprev_x, vnext_x, vprev_y, vnext_y = flow_near
    flow_x = flow[0]
    flow_y = flow[1]
    grad_xx = 0.5 * (vnext_x[0] - vprev_x[0])
    grad_xy = 0.5 * (vnext_y[0] - vprev_y[0])
    grad_yx = 0.5 * (vnext_x[1] - vprev_x[1])
    grad_yy = 0.5 * (vnext_y[1] - vprev_y[1])
    grad_zz = -(grad_xx + grad_yy)
    strain_xy = 0.5 * (grad_xy + grad_yx)
    spin_xy = 0.5 * (grad_xy - grad_yx)
    upwind = (
        jnp.maximum(flow_x, 0.0)[:, None, :] * (centre - prev_x)
        + jnp.minimum(flow_x, 0.0)[:, None, :] * (next_x - centre)
        + jnp.maximum(flow_y, 0.0)[:, None, :] * (centre - prev_y)
        + jnp.minimum(flow_y, 0.0)[:, None, :] * (next_y - centre)
    )
    parts = [centre[:, index, :] for index in range(6)]
    orient = [
        [parts[0], parts[3], parts[4]],
        [parts[3], parts[1], parts[5]],
        [parts[4], parts[5], parts[2]],
    ]
    zero = jnp.zeros_like(grad_xx)
    rate = [[grad_xx, strain_xy, zero], [strain_xy, grad_yy, zero], [zero, zero, grad_zz]]
    spin = [[zero, spin_xy, zero], [-spin_xy, zero, zero], [zero, zero, zero]]
    contraction = sum(
        (orient[first][second] * rate[first][second] for first in range(3) for second in range(3))
    )
    shear = jnp.sqrt(
        2.0
        * sum(
            (rate[first][second] * rate[first][second] for first in range(3) for second in range(3))
        )
        + 1.0
    )
    spin_orient = product(spin, orient)
    orient_spin = product(orient, spin)
    rate_orient = product(rate, orient)
    orient_rate = product(orient, rate)
    sources = []
    for first, second in ((0, 0), (1, 1), (2, 2), (0, 1), (0, 2), (1, 2)):
        delta = 1.0 if first == second else 0.0
        sources.append(
            spin_orient[first][second]
            - orient_spin[first][second]
            + shape_factor
            * (
                rate_orient[first][second]
                + orient_rate[first][second]
                - 2.0 * contraction * orient[first][second]
            )
            + 2.0 * interaction * shear * (delta - 3.0 * orient[first][second])
        )
    sources = sources + [grad_xx, grad_yy, strain_xy]
    for first, second in ((0, 0), (1, 1), (0, 1)):
        sources.append(
            2.0
            * shear_modulus
            * (rate[first][second] + fiber_number * contraction * orient[first][second])
        )
    source = jnp.stack(sources, axis=1)
    return centre + time_step * (source - upwind)


def per_device(
    old_states,
    weight_tiles,
    source_block,
    tile_index,
    dest_device,
    dest_block,
    send_count,
    velocity,
):
    flow_near = neighbours(velocity, 1, 2)
    slot_count = source_block.shape[0]
    block_count = old_states.shape[0]
    state_count = old_states.shape[1]
    lane_count = old_states.shape[2]
    tile_rows = velocity.shape[1]
    pieces = contributions(old_states, weight_tiles, source_block, tile_index, send_count, dest_block)
    is_live = jnp.arange(slot_count) < send_count[0]
    width_y = lax.axis_size("gy")
    width_x = lax.axis_size("gx")
    capacity = slot_count // 4
    own_x = lax.axis_index("gx")
    own_y = lax.axis_index("gy")
    step_x = dest_device // width_y - own_x
    step_y = dest_device % width_y - own_y
    direction = (step_x + 1) * 3 + (step_y + 1)
    matches = ((direction[:, None] == jnp.arange(9)[None, :]) & is_live[:, None]).astype(jnp.int32)
    earlier = jnp.cumsum(matches, axis=0) - matches
    position = jnp.sum(earlier * matches, axis=1)
    target = jnp.where(is_live, direction * capacity + position, 9 * capacity)
    placing = target[None, :] == jnp.arange(9 * capacity)[:, None]
    outgoing = jnp.einsum(
        "ps,scn->cpn", placing.astype(jnp.bfloat16), pieces, preferred_element_type=jnp.float32
    ).astype(jnp.bfloat16)
    channels = state_count + 1
    arrived = []
    for move_x in (-1, 0, 1):
        for move_y in (-1, 0, 1):
            begin = ((move_x + 1) * 3 + (move_y + 1)) * capacity
            chunk = outgoing[:, begin:begin + capacity, :]
            if move_x != 0 or move_y != 0:
                pairs = []
                for source_x in range(width_x):
                    for source_y in range(width_y):
                        goal_x = source_x + move_x
                        goal_y = source_y + move_y
                        if 0 <= goal_x < width_x and 0 <= goal_y < width_y:
                            pairs.append((source_x * width_y + source_y, goal_x * width_y + goal_y))
                chunk = lax.ppermute(chunk, ("gx", "gy"), pairs)
            ids = chunk[state_count, :, 0].astype(jnp.int32)
            selector = (jnp.arange(tile_rows)[:, None] == ids[None, :]).astype(jnp.bfloat16)
            arrived.append((selector, chunk[:state_count]))

    def gathered(pick_rows, pick_lanes):
        total = None
        for selector, data in arrived:
            part = jnp.einsum(
                "rp,cpn->rcn",
                pick_rows(selector),
                pick_lanes(data),
                preferred_element_type=jnp.float32,
            )
            total = part if total is None else total + part
        return total

    edge_rows = gathered(
        lambda sel: jnp.concatenate([sel[:1], sel[-1:]], axis=0), lambda data: data
    )
    edge_cols = gathered(
        lambda sel: sel, lambda data: jnp.concatenate([data[:, :, :1], data[:, :, -1:]], axis=2)
    )
    remapped = gathered(lambda sel: sel, lambda data: data)
    state_near = assemble(
        remapped,
        0,
        2,
        edge_rows[0:1],
        edge_rows[1:2],
        edge_cols[:, :, 0].T,
        edge_cols[:, :, 1].T,
    )
    return advance(remapped, state_near, velocity, flow_near)


def solution(mesh):
    in_specs = (
        P(("gx", "gy"), None, None),
        P(("gx", "gy"), None, None),
        P(("gx", "gy")),
        P(("gx", "gy")),
        P(("gx", "gy")),
        P(("gx", "gy")),
        P(("gx", "gy")),
        P(None, "gx", "gy"),
    )
    out_specs = P("gx", None, "gy")
    return jax.shard_map(
        per_device, mesh=mesh, in_specs=in_specs, out_specs=out_specs, check_vma=False
    )
```

```python
import jax
import jax.numpy as jnp
from jax import lax
from jax.sharding import PartitionSpec as P
from jax.experimental import pallas as pl
from jax.experimental.pallas import tpu as pltpu

time_step = 0.2
shape_factor = 0.95
interaction = 0.01
shear_modulus = 1.0
fiber_number = 2.0


GROUP = 64


def contribution_kernel(tile_ref, source_ref, count_ref, label_ref, old_ref, weight_hbm, out_ref, weight_buf, sems):
    step = pl.program_id(0)
    steps = pl.num_programs(0)

    def fetch(chunk, slot):
        for member in range(GROUP):
            tile = tile_ref[chunk * GROUP + member]
            pltpu.make_async_copy(
                weight_hbm.at[tile], weight_buf.at[slot, member], sems.at[slot, member]
            ).start()

    @pl.when(step == 0)
    def _():
        fetch(0, 0)

    @pl.when(step + 1 < steps)
    def _():
        fetch(step + 1, (step + 1) % 2)

    slot = step % 2
    for member in range(GROUP):
        pltpu.make_async_copy(
            weight_hbm.at[0], weight_buf.at[slot, member], sems.at[slot, member]
        ).wait()
    count = count_ref[0]
    for member in range(GROUP):
        index = step * GROUP + member
        block = old_ref[source_ref[index]]
        weight = weight_buf[slot, member]
        piece = lax.dot_general(
            block, weight, (((1,), (1,)), ((), ())), preferred_element_type=jnp.float32
        )
        piece = jnp.where(index < count, piece, 0.0)
        states = piece.shape[0]
        out_ref[member, pl.ds(0, states), :] = piece.astype(out_ref.dtype)
        tag = jnp.full((1, piece.shape[1]), label_ref[index].astype(jnp.float32), jnp.float32)
        out_ref[member, pl.ds(states, 1), :] = tag.astype(out_ref.dtype)


def contributions(old_states, weight_tiles, source_block, tile_index, send_count, dest_block):
    slot_count = source_block.shape[0]
    block_count, state_count, lane_count = old_states.shape
    rows = weight_tiles.shape[1]
    grid_spec = pltpu.PrefetchScalarGridSpec(
        num_scalar_prefetch=4,
        grid=(slot_count // GROUP,),
        in_specs=[
            pl.BlockSpec((block_count, state_count, lane_count), lambda i, *_: (0, 0, 0)),
            pl.BlockSpec(memory_space=pl.ANY),
        ],
        out_specs=pl.BlockSpec((GROUP, state_count + 1, rows), lambda i, *_: (i, 0, 0)),
        scratch_shapes=[
            pltpu.VMEM((2, GROUP) + weight_tiles.shape[1:], weight_tiles.dtype),
            pltpu.SemaphoreType.DMA((2, GROUP)),
        ],
    )
    return pl.pallas_call(
        contribution_kernel,
        grid_spec=grid_spec,
        out_shape=jax.ShapeDtypeStruct((slot_count, state_count + 1, rows), jnp.bfloat16),
        compiler_params=pltpu.CompilerParams(dimension_semantics=("arbitrary",)),
    )(tile_index, source_block, send_count, dest_block, old_states, weight_tiles)


def shift_in(value, axis, step):
    count = lax.axis_size(axis)
    pairs = [(source, source + step) for source in range(count) if 0 <= source + step < count]
    return lax.ppermute(value, axis, pairs)


def neighbours(x, dim_x, dim_y):
    length_x = x.shape[dim_x]
    length_y = x.shape[dim_y]
    last_x = lax.slice_in_dim(x, length_x - 1, length_x, axis=dim_x)
    first_x = lax.slice_in_dim(x, 0, 1, axis=dim_x)
    last_y = jnp.moveaxis(lax.index_in_dim(x, length_y - 1, axis=dim_y, keepdims=False), dim_x, -1)
    first_y = jnp.moveaxis(lax.index_in_dim(x, 0, axis=dim_y, keepdims=False), dim_x, -1)
    return assemble(x, dim_x, dim_y, first_x, last_x, first_y, last_y)


def assemble(x, dim_x, dim_y, first_x, last_x, first_y, last_y):
    length_x = x.shape[dim_x]
    length_y = x.shape[dim_y]
    before_x = shift_in(last_x, "gx", 1)
    after_x = shift_in(first_x, "gx", -1)
    before_y = jnp.expand_dims(jnp.moveaxis(shift_in(last_y, "gy", 1), -1, dim_x), dim_y)
    after_y = jnp.expand_dims(jnp.moveaxis(shift_in(first_y, "gy", -1), -1, dim_x), dim_y)
    prev_x = jnp.concatenate([before_x, lax.slice_in_dim(x, 0, length_x - 1, axis=dim_x)], axis=dim_x)
    next_x = jnp.concatenate([lax.slice_in_dim(x, 1, length_x, axis=dim_x), after_x], axis=dim_x)
    prev_y = jnp.concatenate([before_y, lax.slice_in_dim(x, 0, length_y - 1, axis=dim_y)], axis=dim_y)
    next_y = jnp.concatenate([lax.slice_in_dim(x, 1, length_y, axis=dim_y), after_y], axis=dim_y)
    return prev_x, next_x, prev_y, next_y


def product(left, right):
    return [
        [
            sum((left[first][inner] * right[inner][second] for inner in range(3)))
            for second in range(3)
        ]
        for first in range(3)
    ]


def advance(centre, state_near, flow, flow_near):
    prev_x, next_x, prev_y, next_y = state_near
    vprev_x, vnext_x, vprev_y, vnext_y = flow_near
    flow_x = flow[0]
    flow_y = flow[1]
    grad_xx = 0.5 * (vnext_x[0] - vprev_x[0])
    grad_xy = 0.5 * (vnext_y[0] - vprev_y[0])
    grad_yx = 0.5 * (vnext_x[1] - vprev_x[1])
    grad_yy = 0.5 * (vnext_y[1] - vprev_y[1])
    grad_zz = -(grad_xx + grad_yy)
    strain_xy = 0.5 * (grad_xy + grad_yx)
    spin_xy = 0.5 * (grad_xy - grad_yx)
    upwind = (
        jnp.maximum(flow_x, 0.0)[:, None, :] * (centre - prev_x)
        + jnp.minimum(flow_x, 0.0)[:, None, :] * (next_x - centre)
        + jnp.maximum(flow_y, 0.0)[:, None, :] * (centre - prev_y)
        + jnp.minimum(flow_y, 0.0)[:, None, :] * (next_y - centre)
    )
    parts = [centre[:, index, :] for index in range(6)]
    orient = [
        [parts[0], parts[3], parts[4]],
        [parts[3], parts[1], parts[5]],
        [parts[4], parts[5], parts[2]],
    ]
    zero = jnp.zeros_like(grad_xx)
    rate = [[grad_xx, strain_xy, zero], [strain_xy, grad_yy, zero], [zero, zero, grad_zz]]
    spin = [[zero, spin_xy, zero], [-spin_xy, zero, zero], [zero, zero, zero]]
    contraction = sum(
        (orient[first][second] * rate[first][second] for first in range(3) for second in range(3))
    )
    shear = jnp.sqrt(
        2.0
        * sum(
            (rate[first][second] * rate[first][second] for first in range(3) for second in range(3))
        )
        + 1.0
    )
    spin_orient = product(spin, orient)
    orient_spin = product(orient, spin)
    rate_orient = product(rate, orient)
    orient_rate = product(orient, rate)
    sources = []
    for first, second in ((0, 0), (1, 1), (2, 2), (0, 1), (0, 2), (1, 2)):
        delta = 1.0 if first == second else 0.0
        sources.append(
            spin_orient[first][second]
            - orient_spin[first][second]
            + shape_factor
            * (
                rate_orient[first][second]
                + orient_rate[first][second]
                - 2.0 * contraction * orient[first][second]
            )
            + 2.0 * interaction * shear * (delta - 3.0 * orient[first][second])
        )
    sources = sources + [grad_xx, grad_yy, strain_xy]
    for first, second in ((0, 0), (1, 1), (0, 1)):
        sources.append(
            2.0
            * shear_modulus
            * (rate[first][second] + fiber_number * contraction * orient[first][second])
        )
    source = jnp.stack(sources, axis=1)
    return centre + time_step * (source - upwind)


def per_device(
    old_states,
    weight_tiles,
    source_block,
    tile_index,
    dest_device,
    dest_block,
    send_count,
    velocity,
):
    flow_near = neighbours(velocity, 1, 2)
    slot_count = source_block.shape[0]
    block_count = old_states.shape[0]
    state_count = old_states.shape[1]
    lane_count = old_states.shape[2]
    tile_rows = velocity.shape[1]
    pieces = contributions(old_states, weight_tiles, source_block, tile_index, send_count, dest_block)
    is_live = jnp.arange(slot_count) < send_count[0]
    width_y = lax.axis_size("gy")
    width_x = lax.axis_size("gx")
    capacity = slot_count // 4
    own_x = lax.axis_index("gx")
    own_y = lax.axis_index("gy")
    step_x = dest_device // width_y - own_x
    step_y = dest_device % width_y - own_y
    direction = (step_x + 1) * 3 + (step_y + 1)
    matches = ((direction[:, None] == jnp.arange(9)[None, :]) & is_live[:, None]).astype(jnp.int32)
    earlier = jnp.cumsum(matches, axis=0) - matches
    position = jnp.sum(earlier * matches, axis=1)
    target = jnp.where(is_live, direction * capacity + position, 9 * capacity)
    placing = target[None, :] == jnp.arange(9 * capacity)[:, None]
    outgoing = jnp.einsum(
        "ps,scn->cpn", placing.astype(jnp.bfloat16), pieces, preferred_element_type=jnp.float32
    ).astype(jnp.bfloat16)
    channels = state_count + 1
    arrived = []
    for move_x in (-1, 0, 1):
        for move_y in (-1, 0, 1):
            begin = ((move_x + 1) * 3 + (move_y + 1)) * capacity
            chunk = outgoing[:, begin:begin + capacity, :]
            if move_x != 0 or move_y != 0:
                pairs = []
                for source_x in range(width_x):
                    for source_y in range(width_y):
                        goal_x = source_x + move_x
                        goal_y = source_y + move_y
                        if 0 <= goal_x < width_x and 0 <= goal_y < width_y:
                            pairs.append((source_x * width_y + source_y, goal_x * width_y + goal_y))
                chunk = lax.ppermute(chunk, ("gx", "gy"), pairs)
            ids = chunk[state_count, :, 0].astype(jnp.int32)
            selector = (jnp.arange(tile_rows)[:, None] == ids[None, :]).astype(jnp.bfloat16)
            arrived.append((selector, chunk[:state_count]))

    remapped = None
    for selector, data in arrived:
        part = jnp.einsum("rp,cpn->rcn", selector, data, preferred_element_type=jnp.float32)
        remapped = part if remapped is None else remapped + part
    state_near = neighbours(remapped, 0, 2)
    return advance(remapped, state_near, velocity, flow_near)


def solution(mesh):
    in_specs = (
        P(("gx", "gy"), None, None),
        P(("gx", "gy"), None, None),
        P(("gx", "gy")),
        P(("gx", "gy")),
        P(("gx", "gy")),
        P(("gx", "gy")),
        P(("gx", "gy")),
        P(None, "gx", "gy"),
    )
    out_specs = P("gx", None, "gy")
    return jax.shard_map(
        per_device, mesh=mesh, in_specs=in_specs, out_specs=out_specs, check_vma=False
    )
```

```python
import jax
import jax.numpy as jnp
from jax import lax
from jax.sharding import PartitionSpec as P
from jax.experimental import pallas as pl
from jax.experimental.pallas import tpu as pltpu

time_step = 0.2
shape_factor = 0.95
interaction = 0.01
shear_modulus = 1.0
fiber_number = 2.0


GROUP = 64


def contribution_kernel(tile_ref, source_ref, count_ref, label_ref, old_ref, weight_hbm, out_ref, weight_buf, sems):
    step = pl.program_id(0)
    steps = pl.num_programs(0)

    def fetch(chunk, slot):
        for member in range(GROUP):
            tile = tile_ref[chunk * GROUP + member]
            pltpu.make_async_copy(
                weight_hbm.at[tile], weight_buf.at[slot, member], sems.at[slot, member]
            ).start()

    @pl.when(step == 0)
    def _():
        fetch(0, 0)

    @pl.when(step + 1 < steps)
    def _():
        fetch(step + 1, (step + 1) % 2)

    slot = step % 2
    for member in range(GROUP):
        pltpu.make_async_copy(
            weight_hbm.at[0], weight_buf.at[slot, member], sems.at[slot, member]
        ).wait()
    count = count_ref[0]
    for member in range(GROUP):
        index = step * GROUP + member
        block = old_ref[source_ref[index]]
        weight = weight_buf[slot, member]
        piece = lax.dot_general(
            block, weight, (((1,), (1,)), ((), ())), preferred_element_type=jnp.float32
        )
        piece = jnp.where(index < count, piece, 0.0)
        states = piece.shape[0]
        out_ref[member, pl.ds(0, states), :] = piece.astype(out_ref.dtype)
        tag = jnp.full((1, piece.shape[1]), label_ref[index].astype(jnp.float32), jnp.float32)
        out_ref[member, pl.ds(states, 1), :] = tag.astype(out_ref.dtype)


def contributions(old_states, weight_tiles, source_block, tile_index, send_count, dest_block):
    slot_count = source_block.shape[0]
    block_count, state_count, lane_count = old_states.shape
    rows = weight_tiles.shape[1]
    grid_spec = pltpu.PrefetchScalarGridSpec(
        num_scalar_prefetch=4,
        grid=(slot_count // GROUP,),
        in_specs=[
            pl.BlockSpec((block_count, state_count, lane_count), lambda i, *_: (0, 0, 0)),
            pl.BlockSpec(memory_space=pl.ANY),
        ],
        out_specs=pl.BlockSpec((GROUP, state_count + 1, rows), lambda i, *_: (i, 0, 0)),
        scratch_shapes=[
            pltpu.VMEM((2, GROUP) + weight_tiles.shape[1:], weight_tiles.dtype),
            pltpu.SemaphoreType.DMA((2, GROUP)),
        ],
    )
    return pl.pallas_call(
        contribution_kernel,
        grid_spec=grid_spec,
        out_shape=jax.ShapeDtypeStruct((slot_count, state_count + 1, rows), jnp.bfloat16),
        compiler_params=pltpu.CompilerParams(dimension_semantics=("arbitrary",)),
    )(tile_index, source_block, send_count, dest_block, old_states, weight_tiles)


def shift_in(value, axis, step):
    count = lax.axis_size(axis)
    pairs = [(source, source + step) for source in range(count) if 0 <= source + step < count]
    return lax.ppermute(value, axis, pairs)


def neighbours(x, dim_x, dim_y):
    length_x = x.shape[dim_x]
    length_y = x.shape[dim_y]
    last_x = lax.slice_in_dim(x, length_x - 1, length_x, axis=dim_x)
    first_x = lax.slice_in_dim(x, 0, 1, axis=dim_x)
    last_y = jnp.moveaxis(lax.index_in_dim(x, length_y - 1, axis=dim_y, keepdims=False), dim_x, -1)
    first_y = jnp.moveaxis(lax.index_in_dim(x, 0, axis=dim_y, keepdims=False), dim_x, -1)
    return assemble(x, dim_x, dim_y, first_x, last_x, first_y, last_y)


def assemble(x, dim_x, dim_y, first_x, last_x, first_y, last_y):
    length_x = x.shape[dim_x]
    length_y = x.shape[dim_y]
    before_x = shift_in(last_x, "gx", 1)
    after_x = shift_in(first_x, "gx", -1)
    before_y = jnp.expand_dims(jnp.moveaxis(shift_in(last_y, "gy", 1), -1, dim_x), dim_y)
    after_y = jnp.expand_dims(jnp.moveaxis(shift_in(first_y, "gy", -1), -1, dim_x), dim_y)
    prev_x = jnp.concatenate([before_x, lax.slice_in_dim(x, 0, length_x - 1, axis=dim_x)], axis=dim_x)
    next_x = jnp.concatenate([lax.slice_in_dim(x, 1, length_x, axis=dim_x), after_x], axis=dim_x)
    prev_y = jnp.concatenate([before_y, lax.slice_in_dim(x, 0, length_y - 1, axis=dim_y)], axis=dim_y)
    next_y = jnp.concatenate([lax.slice_in_dim(x, 1, length_y, axis=dim_y), after_y], axis=dim_y)
    return prev_x, next_x, prev_y, next_y


def product(left, right):
    return [
        [
            sum((left[first][inner] * right[inner][second] for inner in range(3)))
            for second in range(3)
        ]
        for first in range(3)
    ]


def advance(centre, state_near, flow, flow_near):
    prev_x, next_x, prev_y, next_y = state_near
    vprev_x, vnext_x, vprev_y, vnext_y = flow_near
    flow_x = flow[0]
    flow_y = flow[1]
    grad_xx = 0.5 * (vnext_x[0] - vprev_x[0])
    grad_xy = 0.5 * (vnext_y[0] - vprev_y[0])
    grad_yx = 0.5 * (vnext_x[1] - vprev_x[1])
    grad_yy = 0.5 * (vnext_y[1] - vprev_y[1])
    grad_zz = -(grad_xx + grad_yy)
    strain_xy = 0.5 * (grad_xy + grad_yx)
    spin_xy = 0.5 * (grad_xy - grad_yx)
    upwind = (
        jnp.maximum(flow_x, 0.0)[:, None, :] * (centre - prev_x)
        + jnp.minimum(flow_x, 0.0)[:, None, :] * (next_x - centre)
        + jnp.maximum(flow_y, 0.0)[:, None, :] * (centre - prev_y)
        + jnp.minimum(flow_y, 0.0)[:, None, :] * (next_y - centre)
    )
    parts = [centre[:, index, :] for index in range(6)]
    orient = [
        [parts[0], parts[3], parts[4]],
        [parts[3], parts[1], parts[5]],
        [parts[4], parts[5], parts[2]],
    ]
    zero = jnp.zeros_like(grad_xx)
    rate = [[grad_xx, strain_xy, zero], [strain_xy, grad_yy, zero], [zero, zero, grad_zz]]
    spin = [[zero, spin_xy, zero], [-spin_xy, zero, zero], [zero, zero, zero]]
    contraction = sum(
        (orient[first][second] * rate[first][second] for first in range(3) for second in range(3))
    )
    shear = jnp.sqrt(
        2.0
        * sum(
            (rate[first][second] * rate[first][second] for first in range(3) for second in range(3))
        )
        + 1.0
    )
    spin_orient = product(spin, orient)
    orient_spin = product(orient, spin)
    rate_orient = product(rate, orient)
    orient_rate = product(orient, rate)
    sources = []
    for first, second in ((0, 0), (1, 1), (2, 2), (0, 1), (0, 2), (1, 2)):
        delta = 1.0 if first == second else 0.0
        sources.append(
            spin_orient[first][second]
            - orient_spin[first][second]
            + shape_factor
            * (
                rate_orient[first][second]
                + orient_rate[first][second]
                - 2.0 * contraction * orient[first][second]
            )
            + 2.0 * interaction * shear * (delta - 3.0 * orient[first][second])
        )
    sources = sources + [grad_xx, grad_yy, strain_xy]
    for first, second in ((0, 0), (1, 1), (0, 1)):
        sources.append(
            2.0
            * shear_modulus
            * (rate[first][second] + fiber_number * contraction * orient[first][second])
        )
    source = jnp.stack(sources, axis=1)
    return centre + time_step * (source - upwind)


def per_device(
    old_states,
    weight_tiles,
    source_block,
    tile_index,
    dest_device,
    dest_block,
    send_count,
    velocity,
):
    flow_near = neighbours(velocity, 1, 2)
    slot_count = source_block.shape[0]
    block_count = old_states.shape[0]
    state_count = old_states.shape[1]
    lane_count = old_states.shape[2]
    tile_rows = velocity.shape[1]
    pieces = contributions(old_states, weight_tiles, source_block, tile_index, send_count, dest_block)
    is_live = jnp.arange(slot_count) < send_count[0]
    width_y = lax.axis_size("gy")
    width_x = lax.axis_size("gx")
    capacity = slot_count // 4
    own_x = lax.axis_index("gx")
    own_y = lax.axis_index("gy")
    step_x = dest_device // width_y - own_x
    step_y = dest_device % width_y - own_y
    direction = (step_x + 1) * 3 + (step_y + 1)
    matches = ((direction[:, None] == jnp.arange(9)[None, :]) & is_live[:, None]).astype(jnp.int32)
    earlier = jnp.cumsum(matches, axis=0) - matches
    position = jnp.sum(earlier * matches, axis=1)
    target = jnp.where(is_live, direction * capacity + position, 9 * capacity)
    placing = target[None, :] == jnp.arange(9 * capacity)[:, None]
    placing = placing.astype(jnp.bfloat16)
    channels = state_count + 1
    arrived = []
    for move_x in (-1, 0, 1):
        for move_y in (-1, 0, 1):
            begin = ((move_x + 1) * 3 + (move_y + 1)) * capacity
            chunk = jnp.einsum(
                "ps,scn->cpn",
                placing[begin:begin + capacity],
                pieces,
                preferred_element_type=jnp.float32,
            ).astype(jnp.bfloat16)
            if move_x != 0 or move_y != 0:
                pairs = []
                for source_x in range(width_x):
                    for source_y in range(width_y):
                        goal_x = source_x + move_x
                        goal_y = source_y + move_y
                        if 0 <= goal_x < width_x and 0 <= goal_y < width_y:
                            pairs.append((source_x * width_y + source_y, goal_x * width_y + goal_y))
                chunk = lax.ppermute(chunk, ("gx", "gy"), pairs)
            ids = chunk[state_count, :, 0].astype(jnp.int32)
            selector = (jnp.arange(tile_rows)[:, None] == ids[None, :]).astype(jnp.bfloat16)
            arrived.append((selector, chunk[:state_count]))

    remapped = None
    for selector, data in arrived:
        part = jnp.einsum("rp,cpn->rcn", selector, data, preferred_element_type=jnp.float32)
        remapped = part if remapped is None else remapped + part
    flow_near, remapped = lax.optimization_barrier((flow_near, remapped))
    state_near = neighbours(remapped, 0, 2)
    return advance(remapped, state_near, velocity, flow_near)


def solution(mesh):
    in_specs = (
        P(("gx", "gy"), None, None),
        P(("gx", "gy"), None, None),
        P(("gx", "gy")),
        P(("gx", "gy")),
        P(("gx", "gy")),
        P(("gx", "gy")),
        P(("gx", "gy")),
        P(None, "gx", "gy"),
    )
    out_specs = P("gx", None, "gy")
    return jax.shard_map(
        per_device, mesh=mesh, in_specs=in_specs, out_specs=out_specs, check_vma=False
    )
```

```python
import jax
import jax.numpy as jnp
from jax import lax
from jax.sharding import PartitionSpec as P
from jax.experimental import pallas as pl
from jax.experimental.pallas import tpu as pltpu

time_step = 0.2
shape_factor = 0.95
interaction = 0.01
shear_modulus = 1.0
fiber_number = 2.0


GROUP = 64


def contribution_kernel(tile_ref, source_ref, count_ref, label_ref, old_ref, weight_hbm, out_ref, weight_buf, sems):
    step = pl.program_id(0)
    steps = pl.num_programs(0)

    def fetch(chunk, slot):
        for member in range(GROUP):
            tile = tile_ref[chunk * GROUP + member]
            pltpu.make_async_copy(
                weight_hbm.at[tile], weight_buf.at[slot, member], sems.at[slot, member]
            ).start()

    @pl.when(step == 0)
    def _():
        fetch(0, 0)

    @pl.when(step + 1 < steps)
    def _():
        fetch(step + 1, (step + 1) % 2)

    slot = step % 2
    for member in range(GROUP):
        pltpu.make_async_copy(
            weight_hbm.at[0], weight_buf.at[slot, member], sems.at[slot, member]
        ).wait()
    count = count_ref[0]
    for member in range(GROUP):
        index = step * GROUP + member
        block = old_ref[source_ref[index]]
        weight = weight_buf[slot, member]
        piece = lax.dot_general(
            block, weight, (((1,), (1,)), ((), ())), preferred_element_type=jnp.float32
        )
        piece = jnp.where(index < count, piece, 0.0)
        states = piece.shape[0]
        out_ref[member, pl.ds(0, states), :] = piece.astype(out_ref.dtype)
        tag = jnp.full((1, piece.shape[1]), label_ref[index].astype(jnp.float32), jnp.float32)
        out_ref[member, pl.ds(states, 1), :] = tag.astype(out_ref.dtype)


def contributions(old_states, weight_tiles, source_block, tile_index, send_count, dest_block):
    slot_count = source_block.shape[0]
    block_count, state_count, lane_count = old_states.shape
    rows = weight_tiles.shape[1]
    grid_spec = pltpu.PrefetchScalarGridSpec(
        num_scalar_prefetch=4,
        grid=(slot_count // GROUP,),
        in_specs=[
            pl.BlockSpec((block_count, state_count, lane_count), lambda i, *_: (0, 0, 0)),
            pl.BlockSpec(memory_space=pl.ANY),
        ],
        out_specs=pl.BlockSpec((GROUP, state_count + 1, rows), lambda i, *_: (i, 0, 0)),
        scratch_shapes=[
            pltpu.VMEM((2, GROUP) + weight_tiles.shape[1:], weight_tiles.dtype),
            pltpu.SemaphoreType.DMA((2, GROUP)),
        ],
    )
    return pl.pallas_call(
        contribution_kernel,
        grid_spec=grid_spec,
        out_shape=jax.ShapeDtypeStruct((slot_count, state_count + 1, rows), jnp.bfloat16),
        compiler_params=pltpu.CompilerParams(dimension_semantics=("arbitrary",)),
    )(tile_index, source_block, send_count, dest_block, old_states, weight_tiles)


def shift_in(value, axis, step):
    count = lax.axis_size(axis)
    pairs = [(source, source + step) for source in range(count) if 0 <= source + step < count]
    return lax.ppermute(value, axis, pairs)


def neighbours(x, dim_x, dim_y):
    length_x = x.shape[dim_x]
    length_y = x.shape[dim_y]
    last_x = lax.slice_in_dim(x, length_x - 1, length_x, axis=dim_x)
    first_x = lax.slice_in_dim(x, 0, 1, axis=dim_x)
    last_y = jnp.moveaxis(lax.index_in_dim(x, length_y - 1, axis=dim_y, keepdims=False), dim_x, -1)
    first_y = jnp.moveaxis(lax.index_in_dim(x, 0, axis=dim_y, keepdims=False), dim_x, -1)
    return assemble(x, dim_x, dim_y, first_x, last_x, first_y, last_y)


def assemble(x, dim_x, dim_y, first_x, last_x, first_y, last_y):
    length_x = x.shape[dim_x]
    length_y = x.shape[dim_y]
    before_x = shift_in(last_x, "gx", 1)
    after_x = shift_in(first_x, "gx", -1)
    before_y = jnp.expand_dims(jnp.moveaxis(shift_in(last_y, "gy", 1), -1, dim_x), dim_y)
    after_y = jnp.expand_dims(jnp.moveaxis(shift_in(first_y, "gy", -1), -1, dim_x), dim_y)
    prev_x = jnp.concatenate([before_x, lax.slice_in_dim(x, 0, length_x - 1, axis=dim_x)], axis=dim_x)
    next_x = jnp.concatenate([lax.slice_in_dim(x, 1, length_x, axis=dim_x), after_x], axis=dim_x)
    prev_y = jnp.concatenate([before_y, lax.slice_in_dim(x, 0, length_y - 1, axis=dim_y)], axis=dim_y)
    next_y = jnp.concatenate([lax.slice_in_dim(x, 1, length_y, axis=dim_y), after_y], axis=dim_y)
    return prev_x, next_x, prev_y, next_y


def product(left, right):
    return [
        [
            sum((left[first][inner] * right[inner][second] for inner in range(3)))
            for second in range(3)
        ]
        for first in range(3)
    ]


def advance(centre, state_near, flow, flow_near):
    prev_x, next_x, prev_y, next_y = state_near
    vprev_x, vnext_x, vprev_y, vnext_y = flow_near
    flow_x = flow[0]
    flow_y = flow[1]
    grad_xx = 0.5 * (vnext_x[0] - vprev_x[0])
    grad_xy = 0.5 * (vnext_y[0] - vprev_y[0])
    grad_yx = 0.5 * (vnext_x[1] - vprev_x[1])
    grad_yy = 0.5 * (vnext_y[1] - vprev_y[1])
    grad_zz = -(grad_xx + grad_yy)
    strain_xy = 0.5 * (grad_xy + grad_yx)
    spin_xy = 0.5 * (grad_xy - grad_yx)
    upwind = (
        jnp.maximum(flow_x, 0.0)[:, None, :] * (centre - prev_x)
        + jnp.minimum(flow_x, 0.0)[:, None, :] * (next_x - centre)
        + jnp.maximum(flow_y, 0.0)[:, None, :] * (centre - prev_y)
        + jnp.minimum(flow_y, 0.0)[:, None, :] * (next_y - centre)
    )
    parts = [centre[:, index, :] for index in range(6)]
    orient = [
        [parts[0], parts[3], parts[4]],
        [parts[3], parts[1], parts[5]],
        [parts[4], parts[5], parts[2]],
    ]
    zero = jnp.zeros_like(grad_xx)
    rate = [[grad_xx, strain_xy, zero], [strain_xy, grad_yy, zero], [zero, zero, grad_zz]]
    spin = [[zero, spin_xy, zero], [-spin_xy, zero, zero], [zero, zero, zero]]
    contraction = sum(
        (orient[first][second] * rate[first][second] for first in range(3) for second in range(3))
    )
    shear = jnp.sqrt(
        2.0
        * sum(
            (rate[first][second] * rate[first][second] for first in range(3) for second in range(3))
        )
        + 1.0
    )
    spin_orient = product(spin, orient)
    orient_spin = product(orient, spin)
    rate_orient = product(rate, orient)
    orient_rate = product(orient, rate)
    sources = []
    for first, second in ((0, 0), (1, 1), (2, 2), (0, 1), (0, 2), (1, 2)):
        delta = 1.0 if first == second else 0.0
        sources.append(
            spin_orient[first][second]
            - orient_spin[first][second]
            + shape_factor
            * (
                rate_orient[first][second]
                + orient_rate[first][second]
                - 2.0 * contraction * orient[first][second]
            )
            + 2.0 * interaction * shear * (delta - 3.0 * orient[first][second])
        )
    sources = sources + [grad_xx, grad_yy, strain_xy]
    for first, second in ((0, 0), (1, 1), (0, 1)):
        sources.append(
            2.0
            * shear_modulus
            * (rate[first][second] + fiber_number * contraction * orient[first][second])
        )
    source = jnp.stack(sources, axis=1)
    return centre + time_step * (source - upwind)


def per_device(
    old_states,
    weight_tiles,
    source_block,
    tile_index,
    dest_device,
    dest_block,
    send_count,
    velocity,
):
    flow_near = neighbours(velocity, 1, 2)
    slot_count = source_block.shape[0]
    block_count = old_states.shape[0]
    state_count = old_states.shape[1]
    lane_count = old_states.shape[2]
    tile_rows = velocity.shape[1]
    pieces = contributions(old_states, weight_tiles, source_block, tile_index, send_count, dest_block)
    is_live = jnp.arange(slot_count) < send_count[0]
    width_y = lax.axis_size("gy")
    width_x = lax.axis_size("gx")
    capacity = slot_count // 4
    own_x = lax.axis_index("gx")
    own_y = lax.axis_index("gy")
    step_x = dest_device // width_y - own_x
    step_y = dest_device % width_y - own_y
    direction = (step_x + 1) * 3 + (step_y + 1)
    matches = ((direction[:, None] == jnp.arange(9)[None, :]) & is_live[:, None]).astype(jnp.int32)
    earlier = jnp.cumsum(matches, axis=0) - matches
    position = jnp.sum(earlier * matches, axis=1)
    target = jnp.where(is_live, direction * capacity + position, 9 * capacity)
    placing = target[None, :] == jnp.arange(9 * capacity)[:, None]
    outgoing = jnp.einsum(
        "ps,scn->cpn", placing.astype(jnp.bfloat16), pieces, preferred_element_type=jnp.float32
    ).astype(jnp.bfloat16)
    channels = state_count + 1
    arrived = []
    for move_x in (-1, 0, 1):
        for move_y in (-1, 0, 1):
            begin = ((move_x + 1) * 3 + (move_y + 1)) * capacity
            chunk = outgoing[:, begin:begin + capacity, :]
            if move_x != 0 or move_y != 0:
                pairs = []
                for source_x in range(width_x):
                    for source_y in range(width_y):
                        goal_x = source_x + move_x
                        goal_y = source_y + move_y
                        if 0 <= goal_x < width_x and 0 <= goal_y < width_y:
                            pairs.append((source_x * width_y + source_y, goal_x * width_y + goal_y))
                chunk = lax.ppermute(chunk, ("gx", "gy"), pairs)
            arrived.append(chunk)
    arrived = jnp.concatenate(arrived, axis=1)
    ids = arrived[state_count, :, 0].astype(jnp.int32)
    selector = (jnp.arange(tile_rows)[:, None] == ids[None, :]).astype(jnp.bfloat16)
    remapped = jnp.einsum(
        "rp,cpn->rcn", selector, arrived[:state_count], preferred_element_type=jnp.float32
    )
    state_near = neighbours(remapped, 0, 2)
    return advance(remapped, state_near, velocity, flow_near)


def solution(mesh):
    in_specs = (
        P(("gx", "gy"), None, None),
        P(("gx", "gy"), None, None),
        P(("gx", "gy")),
        P(("gx", "gy")),
        P(("gx", "gy")),
        P(("gx", "gy")),
        P(("gx", "gy")),
        P(None, "gx", "gy"),
    )
    out_specs = P("gx", None, "gy")
    return jax.shard_map(
        per_device, mesh=mesh, in_specs=in_specs, out_specs=out_specs, check_vma=False
    )
```

```python
import jax
import jax.numpy as jnp
from jax import lax
from jax.sharding import PartitionSpec as P
from jax.experimental import pallas as pl
from jax.experimental.pallas import tpu as pltpu

time_step = 0.2
shape_factor = 0.95
interaction = 0.01
shear_modulus = 1.0
fiber_number = 2.0


GROUP = 64


def contribution_kernel(tile_ref, source_ref, count_ref, old_ref, weight_hbm, out_ref, weight_buf, sems):
    step = pl.program_id(0)
    steps = pl.num_programs(0)

    def fetch(chunk, slot):
        for member in range(GROUP):
            tile = tile_ref[chunk * GROUP + member]
            pltpu.make_async_copy(
                weight_hbm.at[tile], weight_buf.at[slot, member], sems.at[slot, member]
            ).start()

    @pl.when(step == 0)
    def _():
        fetch(0, 0)

    @pl.when(step + 1 < steps)
    def _():
        fetch(step + 1, (step + 1) % 2)

    slot = step % 2
    for member in range(GROUP):
        pltpu.make_async_copy(
            weight_hbm.at[0], weight_buf.at[slot, member], sems.at[slot, member]
        ).wait()
    count = count_ref[0]
    for member in range(GROUP):
        index = step * GROUP + member
        block = old_ref[source_ref[index]]
        weight = weight_buf[slot, member]
        piece = lax.dot_general(
            block, weight, (((1,), (1,)), ((), ())), preferred_element_type=jnp.float32
        )
        piece = jnp.where(index < count, piece, 0.0)
        out_ref[member] = piece.astype(out_ref.dtype)


def contributions(old_states, weight_tiles, source_block, tile_index, send_count):
    slot_count = source_block.shape[0]
    block_count, state_count, lane_count = old_states.shape
    rows = weight_tiles.shape[1]
    grid_spec = pltpu.PrefetchScalarGridSpec(
        num_scalar_prefetch=3,
        grid=(slot_count // GROUP,),
        in_specs=[
            pl.BlockSpec((block_count, state_count, lane_count), lambda i, *_: (0, 0, 0)),
            pl.BlockSpec(memory_space=pl.ANY),
        ],
        out_specs=pl.BlockSpec((GROUP, state_count, rows), lambda i, *_: (i, 0, 0)),
        scratch_shapes=[
            pltpu.VMEM((2, GROUP) + weight_tiles.shape[1:], weight_tiles.dtype),
            pltpu.SemaphoreType.DMA((2, GROUP)),
        ],
    )
    return pl.pallas_call(
        contribution_kernel,
        grid_spec=grid_spec,
        out_shape=jax.ShapeDtypeStruct((slot_count, state_count, rows), jnp.bfloat16),
        compiler_params=pltpu.CompilerParams(dimension_semantics=("arbitrary",)),
    )(tile_index, source_block, send_count, old_states, weight_tiles)


def shift_in(value, axis, step):
    count = lax.axis_size(axis)
    pairs = [(source, source + step) for source in range(count) if 0 <= source + step < count]
    return lax.ppermute(value, axis, pairs)


def neighbours(x, dim_x, dim_y):
    length_x = x.shape[dim_x]
    length_y = x.shape[dim_y]
    last_x = lax.slice_in_dim(x, length_x - 1, length_x, axis=dim_x)
    first_x = lax.slice_in_dim(x, 0, 1, axis=dim_x)
    last_y = jnp.moveaxis(lax.index_in_dim(x, length_y - 1, axis=dim_y, keepdims=False), dim_x, -1)
    first_y = jnp.moveaxis(lax.index_in_dim(x, 0, axis=dim_y, keepdims=False), dim_x, -1)
    return assemble(x, dim_x, dim_y, first_x, last_x, first_y, last_y)


def assemble(x, dim_x, dim_y, first_x, last_x, first_y, last_y):
    length_x = x.shape[dim_x]
    length_y = x.shape[dim_y]
    before_x = shift_in(last_x, "gx", 1)
    after_x = shift_in(first_x, "gx", -1)
    before_y = jnp.expand_dims(jnp.moveaxis(shift_in(last_y, "gy", 1), -1, dim_x), dim_y)
    after_y = jnp.expand_dims(jnp.moveaxis(shift_in(first_y, "gy", -1), -1, dim_x), dim_y)
    prev_x = jnp.concatenate([before_x, lax.slice_in_dim(x, 0, length_x - 1, axis=dim_x)], axis=dim_x)
    next_x = jnp.concatenate([lax.slice_in_dim(x, 1, length_x, axis=dim_x), after_x], axis=dim_x)
    prev_y = jnp.concatenate([before_y, lax.slice_in_dim(x, 0, length_y - 1, axis=dim_y)], axis=dim_y)
    next_y = jnp.concatenate([lax.slice_in_dim(x, 1, length_y, axis=dim_y), after_y], axis=dim_y)
    return prev_x, next_x, prev_y, next_y


def product(left, right):
    return [
        [
            sum((left[first][inner] * right[inner][second] for inner in range(3)))
            for second in range(3)
        ]
        for first in range(3)
    ]


def advance(centre, state_near, flow, flow_near):
    prev_x, next_x, prev_y, next_y = state_near
    vprev_x, vnext_x, vprev_y, vnext_y = flow_near
    flow_x = flow[0]
    flow_y = flow[1]
    grad_xx = 0.5 * (vnext_x[0] - vprev_x[0])
    grad_xy = 0.5 * (vnext_y[0] - vprev_y[0])
    grad_yx = 0.5 * (vnext_x[1] - vprev_x[1])
    grad_yy = 0.5 * (vnext_y[1] - vprev_y[1])
    grad_zz = -(grad_xx + grad_yy)
    strain_xy = 0.5 * (grad_xy + grad_yx)
    spin_xy = 0.5 * (grad_xy - grad_yx)
    upwind = (
        jnp.maximum(flow_x, 0.0)[:, None, :] * (centre - prev_x)
        + jnp.minimum(flow_x, 0.0)[:, None, :] * (next_x - centre)
        + jnp.maximum(flow_y, 0.0)[:, None, :] * (centre - prev_y)
        + jnp.minimum(flow_y, 0.0)[:, None, :] * (next_y - centre)
    )
    parts = [centre[:, index, :] for index in range(6)]
    orient = [
        [parts[0], parts[3], parts[4]],
        [parts[3], parts[1], parts[5]],
        [parts[4], parts[5], parts[2]],
    ]
    zero = jnp.zeros_like(grad_xx)
    rate = [[grad_xx, strain_xy, zero], [strain_xy, grad_yy, zero], [zero, zero, grad_zz]]
    spin = [[zero, spin_xy, zero], [-spin_xy, zero, zero], [zero, zero, zero]]
    contraction = sum(
        (orient[first][second] * rate[first][second] for first in range(3) for second in range(3))
    )
    shear = jnp.sqrt(
        2.0
        * sum(
            (rate[first][second] * rate[first][second] for first in range(3) for second in range(3))
        )
        + 1.0
    )
    spin_orient = product(spin, orient)
    orient_spin = product(orient, spin)
    rate_orient = product(rate, orient)
    orient_rate = product(orient, rate)
    sources = []
    for first, second in ((0, 0), (1, 1), (2, 2), (0, 1), (0, 2), (1, 2)):
        delta = 1.0 if first == second else 0.0
        sources.append(
            spin_orient[first][second]
            - orient_spin[first][second]
            + shape_factor
            * (
                rate_orient[first][second]
                + orient_rate[first][second]
                - 2.0 * contraction * orient[first][second]
            )
            + 2.0 * interaction * shear * (delta - 3.0 * orient[first][second])
        )
    sources = sources + [grad_xx, grad_yy, strain_xy]
    for first, second in ((0, 0), (1, 1), (0, 1)):
        sources.append(
            2.0
            * shear_modulus
            * (rate[first][second] + fiber_number * contraction * orient[first][second])
        )
    source = jnp.stack(sources, axis=1)
    return centre + time_step * (source - upwind)


def per_device(
    old_states,
    weight_tiles,
    source_block,
    tile_index,
    dest_device,
    dest_block,
    send_count,
    velocity,
):
    flow_near = neighbours(velocity, 1, 2)
    slot_count = source_block.shape[0]
    block_count = old_states.shape[0]
    state_count = old_states.shape[1]
    lane_count = old_states.shape[2]
    tile_rows = velocity.shape[1]
    pieces = contributions(old_states, weight_tiles, source_block, tile_index, send_count)
    is_live = jnp.arange(slot_count) < send_count[0]
    width_y = lax.axis_size("gy")
    width_x = lax.axis_size("gx")
    capacity = slot_count // 4
    own_x = lax.axis_index("gx")
    own_y = lax.axis_index("gy")
    step_x = dest_device // width_y - own_x
    step_y = dest_device % width_y - own_y
    direction = (step_x + 1) * 3 + (step_y + 1)
    matches = ((direction[:, None] == jnp.arange(9)[None, :]) & is_live[:, None]).astype(jnp.int32)
    earlier = jnp.cumsum(matches, axis=0) - matches
    position = jnp.sum(earlier * matches, axis=1)
    target = jnp.where(is_live, direction * capacity + position, 9 * capacity)
    placing = target[None, :] == jnp.arange(9 * capacity)[:, None]
    outgoing = jnp.einsum(
        "ps,scn->cpn", placing.astype(jnp.bfloat16), pieces, preferred_element_type=jnp.float32
    ).astype(jnp.bfloat16)
    labels = jnp.sum(jnp.where(placing, dest_block[None, :], 0), axis=1).astype(jnp.bfloat16)
    label_rows = -(-capacity // lane_count)
    arrived = []
    arrived_ids = []
    for move_x in (-1, 0, 1):
        for move_y in (-1, 0, 1):
            begin = ((move_x + 1) * 3 + (move_y + 1)) * capacity
            chunk = jnp.concatenate(
                [
                    outgoing[:, begin:begin + capacity, :].reshape(state_count * capacity, lane_count),
                    jnp.pad(
                        labels[begin:begin + capacity], (0, label_rows * lane_count - capacity)
                    ).reshape(label_rows, lane_count),
                ],
                axis=0,
            )
            if move_x != 0 or move_y != 0:
                pairs = []
                for source_x in range(width_x):
                    for source_y in range(width_y):
                        goal_x = source_x + move_x
                        goal_y = source_y + move_y
                        if 0 <= goal_x < width_x and 0 <= goal_y < width_y:
                            pairs.append((source_x * width_y + source_y, goal_x * width_y + goal_y))
                chunk = lax.ppermute(chunk, ("gx", "gy"), pairs)
            arrived.append(chunk[: state_count * capacity].reshape(state_count, capacity, lane_count))
            arrived_ids.append(chunk[state_count * capacity:].reshape(-1)[:capacity])
    arrived = jnp.concatenate(arrived, axis=1)
    ids = jnp.concatenate(arrived_ids).astype(jnp.int32)
    selector = (jnp.arange(tile_rows)[:, None] == ids[None, :]).astype(jnp.bfloat16)
    remapped = jnp.einsum("rp,cpn->rcn", selector, arrived, preferred_element_type=jnp.float32)
    state_near = neighbours(remapped, 0, 2)
    return advance(remapped, state_near, velocity, flow_near)


def solution(mesh):
    in_specs = (
        P(("gx", "gy"), None, None),
        P(("gx", "gy"), None, None),
        P(("gx", "gy")),
        P(("gx", "gy")),
        P(("gx", "gy")),
        P(("gx", "gy")),
        P(("gx", "gy")),
        P(None, "gx", "gy"),
    )
    out_specs = P("gx", None, "gy")
    return jax.shard_map(
        per_device, mesh=mesh, in_specs=in_specs, out_specs=out_specs, check_vma=False
    )
```

```python
import jax
import jax.numpy as jnp
from jax import lax
from jax.sharding import PartitionSpec as P
from jax.experimental import pallas as pl
from jax.experimental.pallas import tpu as pltpu

time_step = 0.2
shape_factor = 0.95
interaction = 0.01
shear_modulus = 1.0
fiber_number = 2.0


GROUP = 128


def contribution_kernel(tile_ref, source_ref, count_ref, label_ref, old_ref, weight_hbm, out_ref, weight_buf, sems):
    step = pl.program_id(0)
    steps = pl.num_programs(0)

    def fetch(chunk, slot):
        for member in range(GROUP):
            tile = tile_ref[chunk * GROUP + member]
            pltpu.make_async_copy(
                weight_hbm.at[tile], weight_buf.at[slot, member], sems.at[slot, member]
            ).start()

    @pl.when(step == 0)
    def _():
        fetch(0, 0)

    @pl.when(step + 1 < steps)
    def _():
        fetch(step + 1, (step + 1) % 2)

    slot = step % 2
    for member in range(GROUP):
        pltpu.make_async_copy(
            weight_hbm.at[0], weight_buf.at[slot, member], sems.at[slot, member]
        ).wait()
    count = count_ref[0]
    for member in range(GROUP):
        index = step * GROUP + member
        block = old_ref[source_ref[index]]
        weight = weight_buf[slot, member]
        piece = lax.dot_general(
            block, weight, (((1,), (1,)), ((), ())), preferred_element_type=jnp.float32
        )
        piece = jnp.where(index < count, piece, 0.0)
        states = piece.shape[0]
        out_ref[member, pl.ds(0, states), :] = piece.astype(out_ref.dtype)
        tag = jnp.full((1, piece.shape[1]), label_ref[index].astype(jnp.float32), jnp.float32)
        out_ref[member, pl.ds(states, 1), :] = tag.astype(out_ref.dtype)


def contributions(old_states, weight_tiles, source_block, tile_index, send_count, dest_block):
    slot_count = source_block.shape[0]
    block_count, state_count, lane_count = old_states.shape
    rows = weight_tiles.shape[1]
    grid_spec = pltpu.PrefetchScalarGridSpec(
        num_scalar_prefetch=4,
        grid=(slot_count // GROUP,),
        in_specs=[
            pl.BlockSpec((block_count, state_count, lane_count), lambda i, *_: (0, 0, 0)),
            pl.BlockSpec(memory_space=pl.ANY),
        ],
        out_specs=pl.BlockSpec((GROUP, state_count + 1, rows), lambda i, *_: (i, 0, 0)),
        scratch_shapes=[
            pltpu.VMEM((2, GROUP) + weight_tiles.shape[1:], weight_tiles.dtype),
            pltpu.SemaphoreType.DMA((2, GROUP)),
        ],
    )
    return pl.pallas_call(
        contribution_kernel,
        grid_spec=grid_spec,
        out_shape=jax.ShapeDtypeStruct((slot_count, state_count + 1, rows), jnp.bfloat16),
        compiler_params=pltpu.CompilerParams(dimension_semantics=("arbitrary",)),
    )(tile_index, source_block, send_count, dest_block, old_states, weight_tiles)


def shift_in(value, axis, step):
    count = lax.axis_size(axis)
    pairs = [(source, source + step) for source in range(count) if 0 <= source + step < count]
    return lax.ppermute(value, axis, pairs)


def neighbours(x, dim_x, dim_y):
    length_x = x.shape[dim_x]
    length_y = x.shape[dim_y]
    last_x = lax.slice_in_dim(x, length_x - 1, length_x, axis=dim_x)
    first_x = lax.slice_in_dim(x, 0, 1, axis=dim_x)
    last_y = jnp.moveaxis(lax.index_in_dim(x, length_y - 1, axis=dim_y, keepdims=False), dim_x, -1)
    first_y = jnp.moveaxis(lax.index_in_dim(x, 0, axis=dim_y, keepdims=False), dim_x, -1)
    return assemble(x, dim_x, dim_y, first_x, last_x, first_y, last_y)


def assemble(x, dim_x, dim_y, first_x, last_x, first_y, last_y):
    length_x = x.shape[dim_x]
    length_y = x.shape[dim_y]
    before_x = shift_in(last_x, "gx", 1)
    after_x = shift_in(first_x, "gx", -1)
    before_y = jnp.expand_dims(jnp.moveaxis(shift_in(last_y, "gy", 1), -1, dim_x), dim_y)
    after_y = jnp.expand_dims(jnp.moveaxis(shift_in(first_y, "gy", -1), -1, dim_x), dim_y)
    prev_x = jnp.concatenate([before_x, lax.slice_in_dim(x, 0, length_x - 1, axis=dim_x)], axis=dim_x)
    next_x = jnp.concatenate([lax.slice_in_dim(x, 1, length_x, axis=dim_x), after_x], axis=dim_x)
    prev_y = jnp.concatenate([before_y, lax.slice_in_dim(x, 0, length_y - 1, axis=dim_y)], axis=dim_y)
    next_y = jnp.concatenate([lax.slice_in_dim(x, 1, length_y, axis=dim_y), after_y], axis=dim_y)
    return prev_x, next_x, prev_y, next_y


def product(left, right):
    return [
        [
            sum((left[first][inner] * right[inner][second] for inner in range(3)))
            for second in range(3)
        ]
        for first in range(3)
    ]


def advance(centre, state_near, flow, flow_near):
    prev_x, next_x, prev_y, next_y = state_near
    vprev_x, vnext_x, vprev_y, vnext_y = flow_near
    flow_x = flow[0]
    flow_y = flow[1]
    grad_xx = 0.5 * (vnext_x[0] - vprev_x[0])
    grad_xy = 0.5 * (vnext_y[0] - vprev_y[0])
    grad_yx = 0.5 * (vnext_x[1] - vprev_x[1])
    grad_yy = 0.5 * (vnext_y[1] - vprev_y[1])
    grad_zz = -(grad_xx + grad_yy)
    strain_xy = 0.5 * (grad_xy + grad_yx)
    spin_xy = 0.5 * (grad_xy - grad_yx)
    upwind = (
        jnp.maximum(flow_x, 0.0)[:, None, :] * (centre - prev_x)
        + jnp.minimum(flow_x, 0.0)[:, None, :] * (next_x - centre)
        + jnp.maximum(flow_y, 0.0)[:, None, :] * (centre - prev_y)
        + jnp.minimum(flow_y, 0.0)[:, None, :] * (next_y - centre)
    )
    parts = [centre[:, index, :] for index in range(6)]
    orient = [
        [parts[0], parts[3], parts[4]],
        [parts[3], parts[1], parts[5]],
        [parts[4], parts[5], parts[2]],
    ]
    zero = jnp.zeros_like(grad_xx)
    rate = [[grad_xx, strain_xy, zero], [strain_xy, grad_yy, zero], [zero, zero, grad_zz]]
    spin = [[zero, spin_xy, zero], [-spin_xy, zero, zero], [zero, zero, zero]]
    contraction = sum(
        (orient[first][second] * rate[first][second] for first in range(3) for second in range(3))
    )
    shear = jnp.sqrt(
        2.0
        * sum(
            (rate[first][second] * rate[first][second] for first in range(3) for second in range(3))
        )
        + 1.0
    )
    spin_orient = product(spin, orient)
    orient_spin = product(orient, spin)
    rate_orient = product(rate, orient)
    orient_rate = product(orient, rate)
    sources = []
    for first, second in ((0, 0), (1, 1), (2, 2), (0, 1), (0, 2), (1, 2)):
        delta = 1.0 if first == second else 0.0
        sources.append(
            spin_orient[first][second]
            - orient_spin[first][second]
            + shape_factor
            * (
                rate_orient[first][second]
                + orient_rate[first][second]
                - 2.0 * contraction * orient[first][second]
            )
            + 2.0 * interaction * shear * (delta - 3.0 * orient[first][second])
        )
    sources = sources + [grad_xx, grad_yy, strain_xy]
    for first, second in ((0, 0), (1, 1), (0, 1)):
        sources.append(
            2.0
            * shear_modulus
            * (rate[first][second] + fiber_number * contraction * orient[first][second])
        )
    source = jnp.stack(sources, axis=1)
    return centre + time_step * (source - upwind)


def per_device(
    old_states,
    weight_tiles,
    source_block,
    tile_index,
    dest_device,
    dest_block,
    send_count,
    velocity,
):
    flow_near = neighbours(velocity, 1, 2)
    slot_count = source_block.shape[0]
    block_count = old_states.shape[0]
    state_count = old_states.shape[1]
    lane_count = old_states.shape[2]
    tile_rows = velocity.shape[1]
    pieces = contributions(old_states, weight_tiles, source_block, tile_index, send_count, dest_block)
    is_live = jnp.arange(slot_count) < send_count[0]
    width_y = lax.axis_size("gy")
    width_x = lax.axis_size("gx")
    capacity = slot_count // 4
    own_x = lax.axis_index("gx")
    own_y = lax.axis_index("gy")
    step_x = dest_device // width_y - own_x
    step_y = dest_device % width_y - own_y
    direction = (step_x + 1) * 3 + (step_y + 1)
    matches = ((direction[:, None] == jnp.arange(9)[None, :]) & is_live[:, None]).astype(jnp.int32)
    earlier = jnp.cumsum(matches, axis=0) - matches
    position = jnp.sum(earlier * matches, axis=1)
    target = jnp.where(is_live, direction * capacity + position, 9 * capacity)
    placing = target[None, :] == jnp.arange(9 * capacity)[:, None]
    outgoing = jnp.einsum(
        "ps,scn->cpn", placing.astype(jnp.bfloat16), pieces, preferred_element_type=jnp.float32
    ).astype(jnp.bfloat16)
    channels = state_count + 1
    arrived = []
    for move_x in (-1, 0, 1):
        for move_y in (-1, 0, 1):
            begin = ((move_x + 1) * 3 + (move_y + 1)) * capacity
            chunk = outgoing[:, begin:begin + capacity, :]
            if move_x != 0 or move_y != 0:
                pairs = []
                for source_x in range(width_x):
                    for source_y in range(width_y):
                        goal_x = source_x + move_x
                        goal_y = source_y + move_y
                        if 0 <= goal_x < width_x and 0 <= goal_y < width_y:
                            pairs.append((source_x * width_y + source_y, goal_x * width_y + goal_y))
                chunk = lax.ppermute(chunk, ("gx", "gy"), pairs)
            arrived.append(chunk)
    arrived = jnp.concatenate(arrived, axis=1)
    ids = arrived[state_count, :, 0].astype(jnp.int32)
    selector = (jnp.arange(tile_rows)[:, None] == ids[None, :]).astype(jnp.bfloat16)
    remapped = jnp.einsum(
        "rp,cpn->rcn", selector, arrived[:state_count], preferred_element_type=jnp.float32
    )
    state_near = neighbours(remapped, 0, 2)
    return advance(remapped, state_near, velocity, flow_near)


def solution(mesh):
    in_specs = (
        P(("gx", "gy"), None, None),
        P(("gx", "gy"), None, None),
        P(("gx", "gy")),
        P(("gx", "gy")),
        P(("gx", "gy")),
        P(("gx", "gy")),
        P(("gx", "gy")),
        P(None, "gx", "gy"),
    )
    out_specs = P("gx", None, "gy")
    return jax.shard_map(
        per_device, mesh=mesh, in_specs=in_specs, out_specs=out_specs, check_vma=False
    )
```

```python
import jax
import jax.numpy as jnp
from jax import lax
from jax.sharding import PartitionSpec as P
from jax.experimental import pallas as pl
from jax.experimental.pallas import tpu as pltpu

time_step = 0.2
shape_factor = 0.95
interaction = 0.01
shear_modulus = 1.0
fiber_number = 2.0


GROUP = 64


def contribution_kernel(tile_ref, source_ref, count_ref, label_ref, old_ref, weight_hbm, out_ref, weight_buf, sems):
    step = pl.program_id(0)
    steps = pl.num_programs(0)
    rows = weight_hbm.shape[1]

    def copy(chunk, slot, member):
        tile = tile_ref[chunk * GROUP + member]
        return pltpu.make_async_copy(
            weight_hbm.at[tile],
            weight_buf.at[slot, member // 2, pl.ds((member % 2) * rows, rows)],
            sems.at[slot, member],
        )

    def fetch(chunk, slot):
        for member in range(GROUP):
            copy(chunk, slot, member).start()

    @pl.when(step == 0)
    def _():
        fetch(0, 0)

    @pl.when(step + 1 < steps)
    def _():
        fetch(step + 1, (step + 1) % 2)

    slot = step % 2
    for member in range(GROUP):
        copy(step, slot, member).wait()
    count = count_ref[0]
    padded = old_ref.shape[1]
    states = out_ref.shape[1] - 1
    for pair in range(GROUP // 2):
        first = step * GROUP + 2 * pair
        blocks = jnp.concatenate(
            [old_ref[source_ref[first]], old_ref[source_ref[first + 1]]], axis=0
        )
        both = lax.dot_general(
            blocks, weight_buf[slot, pair], (((1,), (1,)), ((), ())), preferred_element_type=jnp.float32
        )
        for half in range(2):
            index = first + half
            piece = both[half * padded:half * padded + states, half * rows:(half + 1) * rows]
            piece = jnp.where(index < count, piece, 0.0)
            out_ref[2 * pair + half, pl.ds(0, states), :] = piece.astype(out_ref.dtype)
            tag = jnp.full((1, rows), label_ref[index].astype(jnp.float32), jnp.float32)
            out_ref[2 * pair + half, pl.ds(states, 1), :] = tag.astype(out_ref.dtype)


def contributions(old_states, weight_tiles, source_block, tile_index, send_count, dest_block):
    slot_count = source_block.shape[0]
    block_count, state_count, lane_count = old_states.shape
    rows = weight_tiles.shape[1]
    padded = -(-state_count // 16) * 16
    old_padded = jnp.pad(old_states, ((0, 0), (0, padded - state_count), (0, 0)))
    grid_spec = pltpu.PrefetchScalarGridSpec(
        num_scalar_prefetch=4,
        grid=(slot_count // GROUP,),
        in_specs=[
            pl.BlockSpec((block_count, padded, lane_count), lambda i, *_: (0, 0, 0)),
            pl.BlockSpec(memory_space=pl.ANY),
        ],
        out_specs=pl.BlockSpec((GROUP, state_count + 1, rows), lambda i, *_: (i, 0, 0)),
        scratch_shapes=[
            pltpu.VMEM((2, GROUP // 2, 2 * rows, weight_tiles.shape[2]), weight_tiles.dtype),
            pltpu.SemaphoreType.DMA((2, GROUP)),
        ],
    )
    return pl.pallas_call(
        contribution_kernel,
        grid_spec=grid_spec,
        out_shape=jax.ShapeDtypeStruct((slot_count, state_count + 1, rows), jnp.bfloat16),
        compiler_params=pltpu.CompilerParams(dimension_semantics=("arbitrary",)),
    )(tile_index, source_block, send_count, dest_block, old_padded, weight_tiles)


def shift_in(value, axis, step):
    count = lax.axis_size(axis)
    pairs = [(source, source + step) for source in range(count) if 0 <= source + step < count]
    return lax.ppermute(value, axis, pairs)


def neighbours(x, dim_x, dim_y):
    length_x = x.shape[dim_x]
    length_y = x.shape[dim_y]
    last_x = lax.slice_in_dim(x, length_x - 1, length_x, axis=dim_x)
    first_x = lax.slice_in_dim(x, 0, 1, axis=dim_x)
    last_y = jnp.moveaxis(lax.index_in_dim(x, length_y - 1, axis=dim_y, keepdims=False), dim_x, -1)
    first_y = jnp.moveaxis(lax.index_in_dim(x, 0, axis=dim_y, keepdims=False), dim_x, -1)
    return assemble(x, dim_x, dim_y, first_x, last_x, first_y, last_y)


def assemble(x, dim_x, dim_y, first_x, last_x, first_y, last_y):
    length_x = x.shape[dim_x]
    length_y = x.shape[dim_y]
    before_x = shift_in(last_x, "gx", 1)
    after_x = shift_in(first_x, "gx", -1)
    before_y = jnp.expand_dims(jnp.moveaxis(shift_in(last_y, "gy", 1), -1, dim_x), dim_y)
    after_y = jnp.expand_dims(jnp.moveaxis(shift_in(first_y, "gy", -1), -1, dim_x), dim_y)
    prev_x = jnp.concatenate([before_x, lax.slice_in_dim(x, 0, length_x - 1, axis=dim_x)], axis=dim_x)
    next_x = jnp.concatenate([lax.slice_in_dim(x, 1, length_x, axis=dim_x), after_x], axis=dim_x)
    prev_y = jnp.concatenate([before_y, lax.slice_in_dim(x, 0, length_y - 1, axis=dim_y)], axis=dim_y)
    next_y = jnp.concatenate([lax.slice_in_dim(x, 1, length_y, axis=dim_y), after_y], axis=dim_y)
    return prev_x, next_x, prev_y, next_y


def product(left, right):
    return [
        [
            sum((left[first][inner] * right[inner][second] for inner in range(3)))
            for second in range(3)
        ]
        for first in range(3)
    ]


def advance(centre, state_near, flow, flow_near):
    prev_x, next_x, prev_y, next_y = state_near
    vprev_x, vnext_x, vprev_y, vnext_y = flow_near
    flow_x = flow[0]
    flow_y = flow[1]
    grad_xx = 0.5 * (vnext_x[0] - vprev_x[0])
    grad_xy = 0.5 * (vnext_y[0] - vprev_y[0])
    grad_yx = 0.5 * (vnext_x[1] - vprev_x[1])
    grad_yy = 0.5 * (vnext_y[1] - vprev_y[1])
    grad_zz = -(grad_xx + grad_yy)
    strain_xy = 0.5 * (grad_xy + grad_yx)
    spin_xy = 0.5 * (grad_xy - grad_yx)
    upwind = (
        jnp.maximum(flow_x, 0.0)[:, None, :] * (centre - prev_x)
        + jnp.minimum(flow_x, 0.0)[:, None, :] * (next_x - centre)
        + jnp.maximum(flow_y, 0.0)[:, None, :] * (centre - prev_y)
        + jnp.minimum(flow_y, 0.0)[:, None, :] * (next_y - centre)
    )
    parts = [centre[:, index, :] for index in range(6)]
    orient = [
        [parts[0], parts[3], parts[4]],
        [parts[3], parts[1], parts[5]],
        [parts[4], parts[5], parts[2]],
    ]
    zero = jnp.zeros_like(grad_xx)
    rate = [[grad_xx, strain_xy, zero], [strain_xy, grad_yy, zero], [zero, zero, grad_zz]]
    spin = [[zero, spin_xy, zero], [-spin_xy, zero, zero], [zero, zero, zero]]
    contraction = sum(
        (orient[first][second] * rate[first][second] for first in range(3) for second in range(3))
    )
    shear = jnp.sqrt(
        2.0
        * sum(
            (rate[first][second] * rate[first][second] for first in range(3) for second in range(3))
        )
        + 1.0
    )
    spin_orient = product(spin, orient)
    orient_spin = product(orient, spin)
    rate_orient = product(rate, orient)
    orient_rate = product(orient, rate)
    sources = []
    for first, second in ((0, 0), (1, 1), (2, 2), (0, 1), (0, 2), (1, 2)):
        delta = 1.0 if first == second else 0.0
        sources.append(
            spin_orient[first][second]
            - orient_spin[first][second]
            + shape_factor
            * (
                rate_orient[first][second]
                + orient_rate[first][second]
                - 2.0 * contraction * orient[first][second]
            )
            + 2.0 * interaction * shear * (delta - 3.0 * orient[first][second])
        )
    sources = sources + [grad_xx, grad_yy, strain_xy]
    for first, second in ((0, 0), (1, 1), (0, 1)):
        sources.append(
            2.0
            * shear_modulus
            * (rate[first][second] + fiber_number * contraction * orient[first][second])
        )
    source = jnp.stack(sources, axis=1)
    return centre + time_step * (source - upwind)


def per_device(
    old_states,
    weight_tiles,
    source_block,
    tile_index,
    dest_device,
    dest_block,
    send_count,
    velocity,
):
    flow_near = neighbours(velocity, 1, 2)
    slot_count = source_block.shape[0]
    block_count = old_states.shape[0]
    state_count = old_states.shape[1]
    lane_count = old_states.shape[2]
    tile_rows = velocity.shape[1]
    pieces = contributions(old_states, weight_tiles, source_block, tile_index, send_count, dest_block)
    is_live = jnp.arange(slot_count) < send_count[0]
    width_y = lax.axis_size("gy")
    width_x = lax.axis_size("gx")
    capacity = slot_count // 4
    own_x = lax.axis_index("gx")
    own_y = lax.axis_index("gy")
    step_x = dest_device // width_y - own_x
    step_y = dest_device % width_y - own_y
    direction = (step_x + 1) * 3 + (step_y + 1)
    matches = ((direction[:, None] == jnp.arange(9)[None, :]) & is_live[:, None]).astype(jnp.int32)
    earlier = jnp.cumsum(matches, axis=0) - matches
    position = jnp.sum(earlier * matches, axis=1)
    target = jnp.where(is_live, direction * capacity + position, 9 * capacity)
    placing = target[None, :] == jnp.arange(9 * capacity)[:, None]
    outgoing = jnp.einsum(
        "ps,scn->cpn", placing.astype(jnp.bfloat16), pieces, preferred_element_type=jnp.float32
    ).astype(jnp.bfloat16)
    channels = state_count + 1
    arrived = []
    for move_x in (-1, 0, 1):
        for move_y in (-1, 0, 1):
            begin = ((move_x + 1) * 3 + (move_y + 1)) * capacity
            chunk = outgoing[:, begin:begin + capacity, :]
            if move_x != 0 or move_y != 0:
                pairs = []
                for source_x in range(width_x):
                    for source_y in range(width_y):
                        goal_x = source_x + move_x
                        goal_y = source_y + move_y
                        if 0 <= goal_x < width_x and 0 <= goal_y < width_y:
                            pairs.append((source_x * width_y + source_y, goal_x * width_y + goal_y))
                chunk = lax.ppermute(chunk, ("gx", "gy"), pairs)
            arrived.append(chunk)
    arrived = jnp.concatenate(arrived, axis=1)
    ids = arrived[state_count, :, 0].astype(jnp.int32)
    selector = (jnp.arange(tile_rows)[:, None] == ids[None, :]).astype(jnp.bfloat16)
    remapped = jnp.einsum(
        "rp,cpn->rcn", selector, arrived[:state_count], preferred_element_type=jnp.float32
    )
    state_near = neighbours(remapped, 0, 2)
    return advance(remapped, state_near, velocity, flow_near)


def solution(mesh):
    in_specs = (
        P(("gx", "gy"), None, None),
        P(("gx", "gy"), None, None),
        P(("gx", "gy")),
        P(("gx", "gy")),
        P(("gx", "gy")),
        P(("gx", "gy")),
        P(("gx", "gy")),
        P(None, "gx", "gy"),
    )
    out_specs = P("gx", None, "gy")
    return jax.shard_map(
        per_device, mesh=mesh, in_specs=in_specs, out_specs=out_specs, check_vma=False
    )
```

```python
import functools

import jax
import jax.numpy as jnp
from jax import lax
from jax.sharding import PartitionSpec as P
from jax.experimental import pallas as pl
from jax.experimental.pallas import tpu as pltpu

time_step = 0.2
shape_factor = 0.95
interaction = 0.01
shear_modulus = 1.0
fiber_number = 2.0


GROUP = 64


def contribution_kernel(
    state_rows, tile_ref, source_ref, count_ref, label_ref, old_ref, weight_hbm, out_ref, weight_buf, sems
):
    step = pl.program_id(0)
    steps = pl.num_programs(0)
    rows = weight_hbm.shape[1]

    def copy(chunk, slot, member):
        tile = tile_ref[chunk * GROUP + member]
        return pltpu.make_async_copy(
            weight_hbm.at[tile],
            weight_buf.at[slot, member // 2, pl.ds((member % 2) * rows, rows)],
            sems.at[slot, member],
        )

    def fetch(chunk, slot):
        for member in range(GROUP):
            copy(chunk, slot, member).start()

    @pl.when(step == 0)
    def _():
        fetch(0, 0)

    @pl.when(step + 1 < steps)
    def _():
        fetch(step + 1, (step + 1) % 2)

    slot = step % 2
    for member in range(GROUP):
        copy(step, slot, member).wait()
    count = count_ref[0]
    padded = old_ref.shape[1]
    states = state_rows
    for pair in range(GROUP // 2):
        first = step * GROUP + 2 * pair
        blocks = jnp.concatenate(
            [old_ref[source_ref[first]], old_ref[source_ref[first + 1]]], axis=0
        )
        both = lax.dot_general(
            blocks, weight_buf[slot, pair], (((1,), (1,)), ((), ())), preferred_element_type=jnp.float32
        )
        for half in range(2):
            index = first + half
            piece = both[half * padded:(half + 1) * padded, half * rows:(half + 1) * rows]
            piece = jnp.where(index < count, piece, 0.0)
            tag = jnp.where(
                lax.broadcasted_iota(jnp.int32, piece.shape, 0) == states,
                label_ref[index].astype(jnp.float32),
                0.0,
            )
            out_ref[2 * pair + half] = (piece + tag).astype(out_ref.dtype)


def contributions(old_states, weight_tiles, source_block, tile_index, send_count, dest_block):
    slot_count = source_block.shape[0]
    block_count, state_count, lane_count = old_states.shape
    rows = weight_tiles.shape[1]
    padded = -(-(state_count + 1) // 16) * 16
    old_padded = jnp.pad(old_states, ((0, 0), (0, padded - state_count), (0, 0)))
    grid_spec = pltpu.PrefetchScalarGridSpec(
        num_scalar_prefetch=4,
        grid=(slot_count // GROUP,),
        in_specs=[
            pl.BlockSpec((block_count, padded, lane_count), lambda i, *_: (0, 0, 0)),
            pl.BlockSpec(memory_space=pl.ANY),
        ],
        out_specs=pl.BlockSpec((GROUP, padded, rows), lambda i, *_: (i, 0, 0)),
        scratch_shapes=[
            pltpu.VMEM((2, GROUP // 2, 2 * rows, weight_tiles.shape[2]), weight_tiles.dtype),
            pltpu.SemaphoreType.DMA((2, GROUP)),
        ],
    )
    return pl.pallas_call(
        functools.partial(contribution_kernel, state_count),
        grid_spec=grid_spec,
        out_shape=jax.ShapeDtypeStruct((slot_count, padded, rows), jnp.bfloat16),
        compiler_params=pltpu.CompilerParams(dimension_semantics=("arbitrary",)),
    )(tile_index, source_block, send_count, dest_block, old_padded, weight_tiles)


def shift_in(value, axis, step):
    count = lax.axis_size(axis)
    pairs = [(source, source + step) for source in range(count) if 0 <= source + step < count]
    return lax.ppermute(value, axis, pairs)


def neighbours(x, dim_x, dim_y):
    length_x = x.shape[dim_x]
    length_y = x.shape[dim_y]
    last_x = lax.slice_in_dim(x, length_x - 1, length_x, axis=dim_x)
    first_x = lax.slice_in_dim(x, 0, 1, axis=dim_x)
    last_y = jnp.moveaxis(lax.index_in_dim(x, length_y - 1, axis=dim_y, keepdims=False), dim_x, -1)
    first_y = jnp.moveaxis(lax.index_in_dim(x, 0, axis=dim_y, keepdims=False), dim_x, -1)
    return assemble(x, dim_x, dim_y, first_x, last_x, first_y, last_y)


def assemble(x, dim_x, dim_y, first_x, last_x, first_y, last_y):
    length_x = x.shape[dim_x]
    length_y = x.shape[dim_y]
    before_x = shift_in(last_x, "gx", 1)
    after_x = shift_in(first_x, "gx", -1)
    before_y = jnp.expand_dims(jnp.moveaxis(shift_in(last_y, "gy", 1), -1, dim_x), dim_y)
    after_y = jnp.expand_dims(jnp.moveaxis(shift_in(first_y, "gy", -1), -1, dim_x), dim_y)
    prev_x = jnp.concatenate([before_x, lax.slice_in_dim(x, 0, length_x - 1, axis=dim_x)], axis=dim_x)
    next_x = jnp.concatenate([lax.slice_in_dim(x, 1, length_x, axis=dim_x), after_x], axis=dim_x)
    prev_y = jnp.concatenate([before_y, lax.slice_in_dim(x, 0, length_y - 1, axis=dim_y)], axis=dim_y)
    next_y = jnp.concatenate([lax.slice_in_dim(x, 1, length_y, axis=dim_y), after_y], axis=dim_y)
    return prev_x, next_x, prev_y, next_y


def product(left, right):
    return [
        [
            sum((left[first][inner] * right[inner][second] for inner in range(3)))
            for second in range(3)
        ]
        for first in range(3)
    ]


def advance(centre, state_near, flow, flow_near):
    prev_x, next_x, prev_y, next_y = state_near
    vprev_x, vnext_x, vprev_y, vnext_y = flow_near
    flow_x = flow[0]
    flow_y = flow[1]
    grad_xx = 0.5 * (vnext_x[0] - vprev_x[0])
    grad_xy = 0.5 * (vnext_y[0] - vprev_y[0])
    grad_yx = 0.5 * (vnext_x[1] - vprev_x[1])
    grad_yy = 0.5 * (vnext_y[1] - vprev_y[1])
    grad_zz = -(grad_xx + grad_yy)
    strain_xy = 0.5 * (grad_xy + grad_yx)
    spin_xy = 0.5 * (grad_xy - grad_yx)
    upwind = (
        jnp.maximum(flow_x, 0.0)[:, None, :] * (centre - prev_x)
        + jnp.minimum(flow_x, 0.0)[:, None, :] * (next_x - centre)
        + jnp.maximum(flow_y, 0.0)[:, None, :] * (centre - prev_y)
        + jnp.minimum(flow_y, 0.0)[:, None, :] * (next_y - centre)
    )
    parts = [centre[:, index, :] for index in range(6)]
    orient = [
        [parts[0], parts[3], parts[4]],
        [parts[3], parts[1], parts[5]],
        [parts[4], parts[5], parts[2]],
    ]
    zero = jnp.zeros_like(grad_xx)
    rate = [[grad_xx, strain_xy, zero], [strain_xy, grad_yy, zero], [zero, zero, grad_zz]]
    spin = [[zero, spin_xy, zero], [-spin_xy, zero, zero], [zero, zero, zero]]
    contraction = sum(
        (orient[first][second] * rate[first][second] for first in range(3) for second in range(3))
    )
    shear = jnp.sqrt(
        2.0
        * sum(
            (rate[first][second] * rate[first][second] for first in range(3) for second in range(3))
        )
        + 1.0
    )
    spin_orient = product(spin, orient)
    orient_spin = product(orient, spin)
    rate_orient = product(rate, orient)
    orient_rate = product(orient, rate)
    sources = []
    for first, second in ((0, 0), (1, 1), (2, 2), (0, 1), (0, 2), (1, 2)):
        delta = 1.0 if first == second else 0.0
        sources.append(
            spin_orient[first][second]
            - orient_spin[first][second]
            + shape_factor
            * (
                rate_orient[first][second]
                + orient_rate[first][second]
                - 2.0 * contraction * orient[first][second]
            )
            + 2.0 * interaction * shear * (delta - 3.0 * orient[first][second])
        )
    sources = sources + [grad_xx, grad_yy, strain_xy]
    for first, second in ((0, 0), (1, 1), (0, 1)):
        sources.append(
            2.0
            * shear_modulus
            * (rate[first][second] + fiber_number * contraction * orient[first][second])
        )
    source = jnp.stack(sources, axis=1)
    return centre + time_step * (source - upwind)


def per_device(
    old_states,
    weight_tiles,
    source_block,
    tile_index,
    dest_device,
    dest_block,
    send_count,
    velocity,
):
    flow_near = neighbours(velocity, 1, 2)
    slot_count = source_block.shape[0]
    block_count = old_states.shape[0]
    state_count = old_states.shape[1]
    lane_count = old_states.shape[2]
    tile_rows = velocity.shape[1]
    pieces = contributions(old_states, weight_tiles, source_block, tile_index, send_count, dest_block)
    pieces = pieces[:, : state_count + 1]
    is_live = jnp.arange(slot_count) < send_count[0]
    width_y = lax.axis_size("gy")
    width_x = lax.axis_size("gx")
    capacity = slot_count // 4
    own_x = lax.axis_index("gx")
    own_y = lax.axis_index("gy")
    step_x = dest_device // width_y - own_x
    step_y = dest_device % width_y - own_y
    direction = (step_x + 1) * 3 + (step_y + 1)
    matches = ((direction[:, None] == jnp.arange(9)[None, :]) & is_live[:, None]).astype(jnp.int32)
    earlier = jnp.cumsum(matches, axis=0) - matches
    position = jnp.sum(earlier * matches, axis=1)
    target = jnp.where(is_live, direction * capacity + position, 9 * capacity)
    placing = target[None, :] == jnp.arange(9 * capacity)[:, None]
    outgoing = jnp.einsum(
        "ps,scn->cpn", placing.astype(jnp.bfloat16), pieces, preferred_element_type=jnp.float32
    ).astype(jnp.bfloat16)
    channels = state_count + 1
    arrived = []
    for move_x in (-1, 0, 1):
        for move_y in (-1, 0, 1):
            begin = ((move_x + 1) * 3 + (move_y + 1)) * capacity
            chunk = outgoing[:, begin:begin + capacity, :]
            if move_x != 0 or move_y != 0:
                pairs = []
                for source_x in range(width_x):
                    for source_y in range(width_y):
                        goal_x = source_x + move_x
                        goal_y = source_y + move_y
                        if 0 <= goal_x < width_x and 0 <= goal_y < width_y:
                            pairs.append((source_x * width_y + source_y, goal_x * width_y + goal_y))
                chunk = lax.ppermute(chunk, ("gx", "gy"), pairs)
            arrived.append(chunk)
    arrived = jnp.concatenate(arrived, axis=1)
    ids = arrived[state_count, :, 0].astype(jnp.int32)
    selector = (jnp.arange(tile_rows)[:, None] == ids[None, :]).astype(jnp.bfloat16)
    remapped = jnp.einsum(
        "rp,cpn->rcn", selector, arrived[:state_count], preferred_element_type=jnp.float32
    )
    state_near = neighbours(remapped, 0, 2)
    return advance(remapped, state_near, velocity, flow_near)


def solution(mesh):
    in_specs = (
        P(("gx", "gy"), None, None),
        P(("gx", "gy"), None, None),
        P(("gx", "gy")),
        P(("gx", "gy")),
        P(("gx", "gy")),
        P(("gx", "gy")),
        P(("gx", "gy")),
        P(None, "gx", "gy"),
    )
    out_specs = P("gx", None, "gy")
    return jax.shard_map(
        per_device, mesh=mesh, in_specs=in_specs, out_specs=out_specs, check_vma=False
    )
```

```python
import functools

import jax
import jax.numpy as jnp
from jax import lax
from jax.sharding import PartitionSpec as P
from jax.experimental import pallas as pl
from jax.experimental.pallas import tpu as pltpu

time_step = 0.2
shape_factor = 0.95
interaction = 0.01
shear_modulus = 1.0
fiber_number = 2.0


GROUP = 64


def contribution_kernel(
    state_rows, tile_ref, source_ref, count_ref, label_ref, old_ref, weight_hbm, out_ref, weight_buf, sems
):
    step = pl.program_id(0)
    steps = pl.num_programs(0)
    rows = weight_hbm.shape[1]

    def copy(chunk, slot, member):
        tile = tile_ref[chunk * GROUP + member]
        return pltpu.make_async_copy(
            weight_hbm.at[tile],
            weight_buf.at[slot, member // 2, pl.ds((member % 2) * rows, rows)],
            sems.at[slot, member],
        )

    def fetch(chunk, slot):
        for member in range(GROUP):
            copy(chunk, slot, member).start()

    @pl.when(step == 0)
    def _():
        fetch(0, 0)

    @pl.when(step + 1 < steps)
    def _():
        fetch(step + 1, (step + 1) % 2)

    slot = step % 2
    for member in range(GROUP):
        copy(step, slot, member).wait()
    count = count_ref[0]
    padded = old_ref.shape[1]
    states = state_rows
    for pair in range(GROUP // 2):
        first = step * GROUP + 2 * pair
        blocks = jnp.concatenate(
            [old_ref[source_ref[first]], old_ref[source_ref[first + 1]]], axis=0
        )
        both = lax.dot_general(
            blocks, weight_buf[slot, pair], (((1,), (1,)), ((), ())), preferred_element_type=jnp.float32
        )
        for half in range(2):
            index = first + half
            piece = both[half * padded:(half + 1) * padded, half * rows:(half + 1) * rows]
            piece = jnp.where(index < count, piece, 0.0)
            tag = jnp.where(
                lax.broadcasted_iota(jnp.int32, piece.shape, 0) == states,
                label_ref[index].astype(jnp.float32),
                0.0,
            )
            out_ref[2 * pair + half] = (piece + tag).astype(out_ref.dtype)


def contributions(old_states, weight_tiles, source_block, tile_index, send_count, dest_block):
    slot_count = source_block.shape[0]
    block_count, state_count, lane_count = old_states.shape
    rows = weight_tiles.shape[1]
    padded = -(-(state_count + 1) // 16) * 16
    old_padded = jnp.pad(old_states, ((0, 0), (0, padded - state_count), (0, 0)))
    grid_spec = pltpu.PrefetchScalarGridSpec(
        num_scalar_prefetch=4,
        grid=(slot_count // GROUP,),
        in_specs=[
            pl.BlockSpec((block_count, padded, lane_count), lambda i, *_: (0, 0, 0)),
            pl.BlockSpec(memory_space=pl.ANY),
        ],
        out_specs=pl.BlockSpec((GROUP, padded, rows), lambda i, *_: (i, 0, 0)),
        scratch_shapes=[
            pltpu.VMEM((2, GROUP // 2, 2 * rows, weight_tiles.shape[2]), weight_tiles.dtype),
            pltpu.SemaphoreType.DMA((2, GROUP)),
        ],
    )
    return pl.pallas_call(
        functools.partial(contribution_kernel, state_count),
        grid_spec=grid_spec,
        out_shape=jax.ShapeDtypeStruct((slot_count, padded, rows), jnp.bfloat16),
        compiler_params=pltpu.CompilerParams(dimension_semantics=("arbitrary",)),
    )(tile_index, source_block, send_count, dest_block, old_padded, weight_tiles)


def shift_in(value, axis, step):
    count = lax.axis_size(axis)
    pairs = [(source, source + step) for source in range(count) if 0 <= source + step < count]
    return lax.ppermute(value, axis, pairs)


def neighbours(x, dim_x, dim_y):
    length_x = x.shape[dim_x]
    length_y = x.shape[dim_y]
    last_x = lax.slice_in_dim(x, length_x - 1, length_x, axis=dim_x)
    first_x = lax.slice_in_dim(x, 0, 1, axis=dim_x)
    last_y = jnp.moveaxis(lax.index_in_dim(x, length_y - 1, axis=dim_y, keepdims=False), dim_x, -1)
    first_y = jnp.moveaxis(lax.index_in_dim(x, 0, axis=dim_y, keepdims=False), dim_x, -1)
    return assemble(x, dim_x, dim_y, first_x, last_x, first_y, last_y)


def assemble(x, dim_x, dim_y, first_x, last_x, first_y, last_y):
    length_x = x.shape[dim_x]
    length_y = x.shape[dim_y]
    before_x = shift_in(last_x, "gx", 1)
    after_x = shift_in(first_x, "gx", -1)
    before_y = jnp.expand_dims(jnp.moveaxis(shift_in(last_y, "gy", 1), -1, dim_x), dim_y)
    after_y = jnp.expand_dims(jnp.moveaxis(shift_in(first_y, "gy", -1), -1, dim_x), dim_y)
    prev_x = jnp.concatenate([before_x, lax.slice_in_dim(x, 0, length_x - 1, axis=dim_x)], axis=dim_x)
    next_x = jnp.concatenate([lax.slice_in_dim(x, 1, length_x, axis=dim_x), after_x], axis=dim_x)
    prev_y = jnp.concatenate([before_y, lax.slice_in_dim(x, 0, length_y - 1, axis=dim_y)], axis=dim_y)
    next_y = jnp.concatenate([lax.slice_in_dim(x, 1, length_y, axis=dim_y), after_y], axis=dim_y)
    return prev_x, next_x, prev_y, next_y


def product(left, right):
    return [
        [
            sum((left[first][inner] * right[inner][second] for inner in range(3)))
            for second in range(3)
        ]
        for first in range(3)
    ]


def advance(centre, state_near, flow, flow_near):
    prev_x, next_x, prev_y, next_y = state_near
    vprev_x, vnext_x, vprev_y, vnext_y = flow_near
    flow_x = flow[0]
    flow_y = flow[1]
    grad_xx = 0.5 * (vnext_x[0] - vprev_x[0])
    grad_xy = 0.5 * (vnext_y[0] - vprev_y[0])
    grad_yx = 0.5 * (vnext_x[1] - vprev_x[1])
    grad_yy = 0.5 * (vnext_y[1] - vprev_y[1])
    grad_zz = -(grad_xx + grad_yy)
    strain_xy = 0.5 * (grad_xy + grad_yx)
    spin_xy = 0.5 * (grad_xy - grad_yx)
    upwind = (
        jnp.maximum(flow_x, 0.0)[:, None, :] * (centre - prev_x)
        + jnp.minimum(flow_x, 0.0)[:, None, :] * (next_x - centre)
        + jnp.maximum(flow_y, 0.0)[:, None, :] * (centre - prev_y)
        + jnp.minimum(flow_y, 0.0)[:, None, :] * (next_y - centre)
    )
    parts = [centre[:, index, :] for index in range(6)]
    orient = [
        [parts[0], parts[3], parts[4]],
        [parts[3], parts[1], parts[5]],
        [parts[4], parts[5], parts[2]],
    ]
    zero = jnp.zeros_like(grad_xx)
    rate = [[grad_xx, strain_xy, zero], [strain_xy, grad_yy, zero], [zero, zero, grad_zz]]
    spin = [[zero, spin_xy, zero], [-spin_xy, zero, zero], [zero, zero, zero]]
    contraction = sum(
        (orient[first][second] * rate[first][second] for first in range(3) for second in range(3))
    )
    shear = jnp.sqrt(
        2.0
        * sum(
            (rate[first][second] * rate[first][second] for first in range(3) for second in range(3))
        )
        + 1.0
    )
    spin_orient = product(spin, orient)
    orient_spin = product(orient, spin)
    rate_orient = product(rate, orient)
    orient_rate = product(orient, rate)
    sources = []
    for first, second in ((0, 0), (1, 1), (2, 2), (0, 1), (0, 2), (1, 2)):
        delta = 1.0 if first == second else 0.0
        sources.append(
            spin_orient[first][second]
            - orient_spin[first][second]
            + shape_factor
            * (
                rate_orient[first][second]
                + orient_rate[first][second]
                - 2.0 * contraction * orient[first][second]
            )
            + 2.0 * interaction * shear * (delta - 3.0 * orient[first][second])
        )
    sources = sources + [grad_xx, grad_yy, strain_xy]
    for first, second in ((0, 0), (1, 1), (0, 1)):
        sources.append(
            2.0
            * shear_modulus
            * (rate[first][second] + fiber_number * contraction * orient[first][second])
        )
    source = jnp.stack(sources, axis=1)
    return centre + time_step * (source - upwind)


def per_device(
    old_states,
    weight_tiles,
    source_block,
    tile_index,
    dest_device,
    dest_block,
    send_count,
    velocity,
):
    flow_near = neighbours(velocity, 1, 2)
    slot_count = source_block.shape[0]
    block_count = old_states.shape[0]
    state_count = old_states.shape[1]
    lane_count = old_states.shape[2]
    tile_rows = velocity.shape[1]
    pieces = contributions(old_states, weight_tiles, source_block, tile_index, send_count, dest_block)
    pieces = pieces[:, : state_count + 1]
    is_live = jnp.arange(slot_count) < send_count[0]
    width_y = lax.axis_size("gy")
    width_x = lax.axis_size("gx")
    capacity = slot_count // 4
    own_x = lax.axis_index("gx")
    own_y = lax.axis_index("gy")
    step_x = dest_device // width_y - own_x
    step_y = dest_device % width_y - own_y
    direction = (step_x + 1) * 3 + (step_y + 1)
    matches = ((direction[:, None] == jnp.arange(9)[None, :]) & is_live[:, None]).astype(jnp.int32)
    earlier = jnp.cumsum(matches, axis=0) - matches
    position = jnp.sum(earlier * matches, axis=1)
    target = jnp.where(is_live, direction * capacity + position, 9 * capacity)
    placing = target[None, :] == jnp.arange(9 * capacity)[:, None]
    outgoing = jnp.einsum(
        "ps,scn->cpn", placing.astype(jnp.bfloat16), pieces, preferred_element_type=jnp.float32
    ).astype(jnp.bfloat16)
    channels = state_count + 1
    arrived = []
    for move_x in (-1, 0, 1):
        for move_y in (-1, 0, 1):
            begin = ((move_x + 1) * 3 + (move_y + 1)) * capacity
            chunk = outgoing[:, begin:begin + capacity, :]
            if move_x != 0 or move_y != 0:
                pairs = []
                for source_x in range(width_x):
                    for source_y in range(width_y):
                        goal_x = source_x + move_x
                        goal_y = source_y + move_y
                        if 0 <= goal_x < width_x and 0 <= goal_y < width_y:
                            pairs.append((source_x * width_y + source_y, goal_x * width_y + goal_y))
                chunk = lax.ppermute(chunk, ("gx", "gy"), pairs)
            arrived.append(chunk)
    arrived = jnp.concatenate(arrived, axis=1)
    ids = arrived[state_count, :, 0].astype(jnp.int32)
    selector = (jnp.arange(tile_rows)[:, None] == ids[None, :]).astype(jnp.bfloat16)
    remapped = jnp.einsum(
        "rp,cpn->rcn", selector, arrived[:state_count], preferred_element_type=jnp.float32
    )
    zero_row = jnp.zeros_like(remapped[:1])
    zero_col = jnp.zeros_like(remapped[:, :, :1])
    zero_near = (
        jnp.concatenate([zero_row, remapped[:-1]], axis=0),
        jnp.concatenate([remapped[1:], zero_row], axis=0),
        jnp.concatenate([zero_col, remapped[:, :, :-1]], axis=2),
        jnp.concatenate([remapped[:, :, 1:], zero_col], axis=2),
    )
    before_x = shift_in(remapped[-1:], "gx", 1)[0]
    after_x = shift_in(remapped[:1], "gx", -1)[0]
    before_y = shift_in(remapped[:, :, -1].T, "gy", 1).T
    after_y = shift_in(remapped[:, :, 0].T, "gy", -1).T
    stepped = advance(remapped, zero_near, velocity, flow_near)
    flow_x = velocity[0]
    flow_y = velocity[1]
    stepped = stepped.at[0].add(time_step * jnp.maximum(flow_x[0], 0.0)[None, :] * before_x)
    stepped = stepped.at[-1].add(-time_step * jnp.minimum(flow_x[-1], 0.0)[None, :] * after_x)
    stepped = stepped.at[:, :, 0].add(time_step * jnp.maximum(flow_y[:, 0], 0.0)[:, None] * before_y)
    stepped = stepped.at[:, :, -1].add(-time_step * jnp.minimum(flow_y[:, -1], 0.0)[:, None] * after_y)
    return stepped


def solution(mesh):
    in_specs = (
        P(("gx", "gy"), None, None),
        P(("gx", "gy"), None, None),
        P(("gx", "gy")),
        P(("gx", "gy")),
        P(("gx", "gy")),
        P(("gx", "gy")),
        P(("gx", "gy")),
        P(None, "gx", "gy"),
    )
    out_specs = P("gx", None, "gy")
    return jax.shard_map(
        per_device, mesh=mesh, in_specs=in_specs, out_specs=out_specs, check_vma=False
    )
```

```python
import functools

import jax
import jax.numpy as jnp
from jax import lax
from jax.sharding import PartitionSpec as P
from jax.experimental import pallas as pl
from jax.experimental.pallas import tpu as pltpu

time_step = 0.2
shape_factor = 0.95
interaction = 0.01
shear_modulus = 1.0
fiber_number = 2.0


GROUP = 64


def contribution_kernel(
    state_rows, tile_ref, source_ref, count_ref, label_ref, old_ref, weight_hbm, out_ref, weight_buf, sems
):
    step = pl.program_id(0)
    steps = pl.num_programs(0)
    rows = weight_hbm.shape[1]

    def copy(chunk, slot, member):
        tile = tile_ref[chunk * GROUP + member]
        return pltpu.make_async_copy(
            weight_hbm.at[tile],
            weight_buf.at[slot, member // 2, pl.ds((member % 2) * rows, rows)],
            sems.at[slot, member],
        )

    def fetch(chunk, slot):
        for member in range(GROUP):
            copy(chunk, slot, member).start()

    @pl.when(step == 0)
    def _():
        fetch(0, 0)

    @pl.when(step + 1 < steps)
    def _():
        fetch(step + 1, (step + 1) % 2)

    slot = step % 2
    for member in range(GROUP):
        copy(step, slot, member).wait()
    count = count_ref[0]
    padded = old_ref.shape[1]
    states = state_rows
    for pair in range(GROUP // 2):
        first = step * GROUP + 2 * pair
        blocks = jnp.concatenate(
            [old_ref[source_ref[first]], old_ref[source_ref[first + 1]]], axis=0
        )
        both = lax.dot_general(
            blocks, weight_buf[slot, pair], (((1,), (1,)), ((), ())), preferred_element_type=jnp.float32
        )
        for half in range(2):
            index = first + half
            piece = both[half * padded:(half + 1) * padded, half * rows:(half + 1) * rows]
            piece = jnp.where(index < count, piece, 0.0)
            tag = jnp.where(
                lax.broadcasted_iota(jnp.int32, piece.shape, 0) == states,
                label_ref[index].astype(jnp.float32),
                0.0,
            )
            out_ref[2 * pair + half] = (piece + tag).astype(out_ref.dtype)


def contributions(old_states, weight_tiles, source_block, tile_index, send_count, dest_block):
    slot_count = source_block.shape[0]
    block_count, state_count, lane_count = old_states.shape
    rows = weight_tiles.shape[1]
    padded = -(-(state_count + 1) // 16) * 16
    old_padded = jnp.pad(old_states, ((0, 0), (0, padded - state_count), (0, 0)))
    grid_spec = pltpu.PrefetchScalarGridSpec(
        num_scalar_prefetch=4,
        grid=(slot_count // GROUP,),
        in_specs=[
            pl.BlockSpec((block_count, padded, lane_count), lambda i, *_: (0, 0, 0)),
            pl.BlockSpec(memory_space=pl.ANY),
        ],
        out_specs=pl.BlockSpec((GROUP, padded, rows), lambda i, *_: (i, 0, 0)),
        scratch_shapes=[
            pltpu.VMEM((2, GROUP // 2, 2 * rows, weight_tiles.shape[2]), weight_tiles.dtype),
            pltpu.SemaphoreType.DMA((2, GROUP)),
        ],
    )
    return pl.pallas_call(
        functools.partial(contribution_kernel, state_count),
        grid_spec=grid_spec,
        out_shape=jax.ShapeDtypeStruct((slot_count, padded, rows), jnp.bfloat16),
        compiler_params=pltpu.CompilerParams(dimension_semantics=("arbitrary",)),
    )(tile_index, source_block, send_count, dest_block, old_padded, weight_tiles)


def shift_in(value, axis, step):
    count = lax.axis_size(axis)
    pairs = [(source, source + step) for source in range(count) if 0 <= source + step < count]
    return lax.ppermute(value, axis, pairs)


def neighbours(x, dim_x, dim_y):
    length_x = x.shape[dim_x]
    length_y = x.shape[dim_y]
    last_x = lax.slice_in_dim(x, length_x - 1, length_x, axis=dim_x)
    first_x = lax.slice_in_dim(x, 0, 1, axis=dim_x)
    last_y = jnp.moveaxis(lax.index_in_dim(x, length_y - 1, axis=dim_y, keepdims=False), dim_x, -1)
    first_y = jnp.moveaxis(lax.index_in_dim(x, 0, axis=dim_y, keepdims=False), dim_x, -1)
    return assemble(x, dim_x, dim_y, first_x, last_x, first_y, last_y)


def assemble(x, dim_x, dim_y, first_x, last_x, first_y, last_y):
    length_x = x.shape[dim_x]
    length_y = x.shape[dim_y]
    before_x = shift_in(last_x, "gx", 1)
    after_x = shift_in(first_x, "gx", -1)
    before_y = jnp.expand_dims(jnp.moveaxis(shift_in(last_y, "gy", 1), -1, dim_x), dim_y)
    after_y = jnp.expand_dims(jnp.moveaxis(shift_in(first_y, "gy", -1), -1, dim_x), dim_y)
    prev_x = jnp.concatenate([before_x, lax.slice_in_dim(x, 0, length_x - 1, axis=dim_x)], axis=dim_x)
    next_x = jnp.concatenate([lax.slice_in_dim(x, 1, length_x, axis=dim_x), after_x], axis=dim_x)
    prev_y = jnp.concatenate([before_y, lax.slice_in_dim(x, 0, length_y - 1, axis=dim_y)], axis=dim_y)
    next_y = jnp.concatenate([lax.slice_in_dim(x, 1, length_y, axis=dim_y), after_y], axis=dim_y)
    return prev_x, next_x, prev_y, next_y


def product(left, right):
    return [
        [
            sum((left[first][inner] * right[inner][second] for inner in range(3)))
            for second in range(3)
        ]
        for first in range(3)
    ]


def advance(centre, state_near, flow, flow_near):
    prev_x, next_x, prev_y, next_y = state_near
    vprev_x, vnext_x, vprev_y, vnext_y = flow_near
    flow_x = flow[0]
    flow_y = flow[1]
    grad_xx = 0.5 * (vnext_x[0] - vprev_x[0])
    grad_xy = 0.5 * (vnext_y[0] - vprev_y[0])
    grad_yx = 0.5 * (vnext_x[1] - vprev_x[1])
    grad_yy = 0.5 * (vnext_y[1] - vprev_y[1])
    grad_zz = -(grad_xx + grad_yy)
    strain_xy = 0.5 * (grad_xy + grad_yx)
    spin_xy = 0.5 * (grad_xy - grad_yx)
    upwind = (
        jnp.maximum(flow_x, 0.0)[:, None, :] * (centre - prev_x)
        + jnp.minimum(flow_x, 0.0)[:, None, :] * (next_x - centre)
        + jnp.maximum(flow_y, 0.0)[:, None, :] * (centre - prev_y)
        + jnp.minimum(flow_y, 0.0)[:, None, :] * (next_y - centre)
    )
    parts = [centre[:, index, :] for index in range(6)]
    orient = [
        [parts[0], parts[3], parts[4]],
        [parts[3], parts[1], parts[5]],
        [parts[4], parts[5], parts[2]],
    ]
    zero = jnp.zeros_like(grad_xx)
    rate = [[grad_xx, strain_xy, zero], [strain_xy, grad_yy, zero], [zero, zero, grad_zz]]
    spin = [[zero, spin_xy, zero], [-spin_xy, zero, zero], [zero, zero, zero]]
    contraction = sum(
        (orient[first][second] * rate[first][second] for first in range(3) for second in range(3))
    )
    shear = jnp.sqrt(
        2.0
        * sum(
            (rate[first][second] * rate[first][second] for first in range(3) for second in range(3))
        )
        + 1.0
    )
    spin_orient = product(spin, orient)
    orient_spin = product(orient, spin)
    rate_orient = product(rate, orient)
    orient_rate = product(orient, rate)
    sources = []
    for first, second in ((0, 0), (1, 1), (2, 2), (0, 1), (0, 2), (1, 2)):
        delta = 1.0 if first == second else 0.0
        sources.append(
            spin_orient[first][second]
            - orient_spin[first][second]
            + shape_factor
            * (
                rate_orient[first][second]
                + orient_rate[first][second]
                - 2.0 * contraction * orient[first][second]
            )
            + 2.0 * interaction * shear * (delta - 3.0 * orient[first][second])
        )
    sources = sources + [grad_xx, grad_yy, strain_xy]
    for first, second in ((0, 0), (1, 1), (0, 1)):
        sources.append(
            2.0
            * shear_modulus
            * (rate[first][second] + fiber_number * contraction * orient[first][second])
        )
    source = jnp.stack(sources, axis=1)
    return centre + time_step * (source - upwind)


def per_device(
    old_states,
    weight_tiles,
    source_block,
    tile_index,
    dest_device,
    dest_block,
    send_count,
    velocity,
):
    flow_near = neighbours(velocity, 1, 2)
    slot_count = source_block.shape[0]
    block_count = old_states.shape[0]
    state_count = old_states.shape[1]
    lane_count = old_states.shape[2]
    tile_rows = velocity.shape[1]
    pieces = contributions(old_states, weight_tiles, source_block, tile_index, send_count, dest_block)
    pieces = pieces[:, : state_count + 1]
    is_live = jnp.arange(slot_count) < send_count[0]
    width_y = lax.axis_size("gy")
    width_x = lax.axis_size("gx")
    capacity = slot_count // 4
    own_x = lax.axis_index("gx")
    own_y = lax.axis_index("gy")
    step_x = dest_device // width_y - own_x
    step_y = dest_device % width_y - own_y
    direction = (step_x + 1) * 3 + (step_y + 1)
    matches = ((direction[:, None] == jnp.arange(9)[None, :]) & is_live[:, None]).astype(jnp.int32)
    earlier = jnp.cumsum(matches, axis=0) - matches
    position = jnp.sum(earlier * matches, axis=1)
    target = jnp.where(is_live, direction * capacity + position, 9 * capacity)
    placing = target[None, :] == jnp.arange(9 * capacity)[:, None]
    outgoing = jnp.einsum(
        "ps,scn->cpn", placing.astype(jnp.bfloat16), pieces, preferred_element_type=jnp.float32
    ).astype(jnp.bfloat16)
    channels = state_count + 1
    arrived = []
    for move_x in (-1, 0, 1):
        for move_y in (-1, 0, 1):
            begin = ((move_x + 1) * 3 + (move_y + 1)) * capacity
            chunk = outgoing[:, begin:begin + capacity, :]
            if move_x != 0 or move_y != 0:
                pairs = []
                for source_x in range(width_x):
                    for source_y in range(width_y):
                        goal_x = source_x + move_x
                        goal_y = source_y + move_y
                        if 0 <= goal_x < width_x and 0 <= goal_y < width_y:
                            pairs.append((source_x * width_y + source_y, goal_x * width_y + goal_y))
                chunk = lax.ppermute(chunk, ("gx", "gy"), pairs)
            arrived.append(chunk)
    arrived = jnp.concatenate(arrived, axis=1)
    ids = arrived[state_count, :, 0].astype(jnp.int32)
    selector = (jnp.arange(tile_rows)[:, None] == ids[None, :]).astype(jnp.bfloat16)
    remapped = jnp.einsum(
        "rp,cpn->rcn", selector, arrived[:state_count], preferred_element_type=jnp.float32
    )
    zero_row = jnp.zeros_like(remapped[:1])
    zero_col = jnp.zeros_like(remapped[:, :, :1])
    zero_near = (
        jnp.concatenate([zero_row, remapped[:-1]], axis=0),
        jnp.concatenate([remapped[1:], zero_row], axis=0),
        jnp.concatenate([zero_col, remapped[:, :, :-1]], axis=2),
        jnp.concatenate([remapped[:, :, 1:], zero_col], axis=2),
    )
    before_x = shift_in(remapped[-1:], "gx", 1)[0]
    after_x = shift_in(remapped[:1], "gx", -1)[0]
    before_y = shift_in(remapped[:, :, -1].T, "gy", 1).T
    after_y = shift_in(remapped[:, :, 0].T, "gy", -1).T
    stepped = advance(remapped, zero_near, velocity, flow_near)
    flow_x = velocity[0]
    flow_y = velocity[1]
    fix_first_row = time_step * jnp.maximum(flow_x[0], 0.0)[None, :] * before_x
    fix_last_row = time_step * jnp.minimum(flow_x[-1], 0.0)[None, :] * after_x
    fix_first_lane = time_step * jnp.maximum(flow_y[:, 0], 0.0)[:, None] * before_y
    fix_last_lane = time_step * jnp.minimum(flow_y[:, -1], 0.0)[:, None] * after_y
    last_row = stepped.shape[0] - 1
    last_lane = stepped.shape[2] - 1
    stepped = lax.dynamic_update_slice(stepped, stepped[:1] + fix_first_row[None], (0, 0, 0))
    stepped = lax.dynamic_update_slice(stepped, stepped[-1:] - fix_last_row[None], (last_row, 0, 0))
    stepped = lax.dynamic_update_slice(
        stepped, stepped[:, :, :1] + fix_first_lane[:, :, None], (0, 0, 0)
    )
    stepped = lax.dynamic_update_slice(
        stepped, stepped[:, :, -1:] - fix_last_lane[:, :, None], (0, 0, last_lane)
    )
    return stepped


def solution(mesh):
    in_specs = (
        P(("gx", "gy"), None, None),
        P(("gx", "gy"), None, None),
        P(("gx", "gy")),
        P(("gx", "gy")),
        P(("gx", "gy")),
        P(("gx", "gy")),
        P(("gx", "gy")),
        P(None, "gx", "gy"),
    )
    out_specs = P("gx", None, "gy")
    return jax.shard_map(
        per_device, mesh=mesh, in_specs=in_specs, out_specs=out_specs, check_vma=False
    )
```

```python
import functools

import jax
import jax.numpy as jnp
from jax import lax
from jax.sharding import PartitionSpec as P
from jax.experimental import pallas as pl
from jax.experimental.pallas import tpu as pltpu

time_step = 0.2
shape_factor = 0.95
interaction = 0.01
shear_modulus = 1.0
fiber_number = 2.0


GROUP = 64


def contribution_kernel(
    state_rows, tile_ref, source_ref, count_ref, label_ref, old_ref, weight_hbm, out_ref, weight_buf, sems
):
    step = pl.program_id(0)
    steps = pl.num_programs(0)
    rows = weight_hbm.shape[1]

    def copy(chunk, slot, member):
        tile = tile_ref[chunk * GROUP + member]
        return pltpu.make_async_copy(
            weight_hbm.at[tile],
            weight_buf.at[slot, member // 2, pl.ds((member % 2) * rows, rows)],
            sems.at[slot, member],
        )

    def fetch(chunk, slot):
        for member in range(GROUP):
            copy(chunk, slot, member).start()

    @pl.when(step == 0)
    def _():
        fetch(0, 0)

    @pl.when(step + 1 < steps)
    def _():
        fetch(step + 1, (step + 1) % 2)

    slot = step % 2
    for member in range(GROUP):
        copy(step, slot, member).wait()
    count = count_ref[0]
    padded = old_ref.shape[1]
    states = state_rows
    for pair in range(GROUP // 2):
        first = step * GROUP + 2 * pair
        blocks = jnp.concatenate(
            [old_ref[source_ref[first]], old_ref[source_ref[first + 1]]], axis=0
        )
        both = lax.dot_general(
            blocks, weight_buf[slot, pair], (((1,), (1,)), ((), ())), preferred_element_type=jnp.float32
        )
        for half in range(2):
            index = first + half
            piece = both[half * padded:(half + 1) * padded, half * rows:(half + 1) * rows]
            piece = jnp.where(index < count, piece, 0.0)
            tag = jnp.where(
                lax.broadcasted_iota(jnp.int32, piece.shape, 0) == states,
                label_ref[index].astype(jnp.float32),
                0.0,
            )
            out_ref[2 * pair + half] = (piece + tag).astype(out_ref.dtype)


def contributions(old_states, weight_tiles, source_block, tile_index, send_count, dest_block):
    slot_count = source_block.shape[0]
    block_count, state_count, lane_count = old_states.shape
    rows = weight_tiles.shape[1]
    padded = -(-(state_count + 1) // 16) * 16
    old_padded = jnp.pad(old_states, ((0, 0), (0, padded - state_count), (0, 0)))
    grid_spec = pltpu.PrefetchScalarGridSpec(
        num_scalar_prefetch=4,
        grid=(slot_count // GROUP,),
        in_specs=[
            pl.BlockSpec((block_count, padded, lane_count), lambda i, *_: (0, 0, 0)),
            pl.BlockSpec(memory_space=pl.ANY),
        ],
        out_specs=pl.BlockSpec((GROUP, padded, rows), lambda i, *_: (i, 0, 0)),
        scratch_shapes=[
            pltpu.VMEM((2, GROUP // 2, 2 * rows, weight_tiles.shape[2]), weight_tiles.dtype),
            pltpu.SemaphoreType.DMA((2, GROUP)),
        ],
    )
    return pl.pallas_call(
        functools.partial(contribution_kernel, state_count),
        grid_spec=grid_spec,
        out_shape=jax.ShapeDtypeStruct((slot_count, padded, rows), jnp.bfloat16),
        compiler_params=pltpu.CompilerParams(dimension_semantics=("arbitrary",)),
    )(tile_index, source_block, send_count, dest_block, old_padded, weight_tiles)


def shift_in(value, axis, step):
    count = lax.axis_size(axis)
    pairs = [(source, source + step) for source in range(count) if 0 <= source + step < count]
    return lax.ppermute(value, axis, pairs)


def neighbours(x, dim_x, dim_y):
    length_x = x.shape[dim_x]
    length_y = x.shape[dim_y]
    last_x = lax.slice_in_dim(x, length_x - 1, length_x, axis=dim_x)
    first_x = lax.slice_in_dim(x, 0, 1, axis=dim_x)
    last_y = jnp.moveaxis(lax.index_in_dim(x, length_y - 1, axis=dim_y, keepdims=False), dim_x, -1)
    first_y = jnp.moveaxis(lax.index_in_dim(x, 0, axis=dim_y, keepdims=False), dim_x, -1)
    return assemble(x, dim_x, dim_y, first_x, last_x, first_y, last_y)


def assemble(x, dim_x, dim_y, first_x, last_x, first_y, last_y):
    length_x = x.shape[dim_x]
    length_y = x.shape[dim_y]
    before_x = shift_in(last_x, "gx", 1)
    after_x = shift_in(first_x, "gx", -1)
    before_y = jnp.expand_dims(jnp.moveaxis(shift_in(last_y, "gy", 1), -1, dim_x), dim_y)
    after_y = jnp.expand_dims(jnp.moveaxis(shift_in(first_y, "gy", -1), -1, dim_x), dim_y)
    prev_x = jnp.concatenate([before_x, lax.slice_in_dim(x, 0, length_x - 1, axis=dim_x)], axis=dim_x)
    next_x = jnp.concatenate([lax.slice_in_dim(x, 1, length_x, axis=dim_x), after_x], axis=dim_x)
    prev_y = jnp.concatenate([before_y, lax.slice_in_dim(x, 0, length_y - 1, axis=dim_y)], axis=dim_y)
    next_y = jnp.concatenate([lax.slice_in_dim(x, 1, length_y, axis=dim_y), after_y], axis=dim_y)
    return prev_x, next_x, prev_y, next_y


def product(left, right):
    return [
        [
            sum((left[first][inner] * right[inner][second] for inner in range(3)))
            for second in range(3)
        ]
        for first in range(3)
    ]


def advance(centre, state_near, flow, flow_near):
    prev_x, next_x, prev_y, next_y = state_near
    vprev_x, vnext_x, vprev_y, vnext_y = flow_near
    flow_x = flow[0]
    flow_y = flow[1]
    grad_xx = 0.5 * (vnext_x[0] - vprev_x[0])
    grad_xy = 0.5 * (vnext_y[0] - vprev_y[0])
    grad_yx = 0.5 * (vnext_x[1] - vprev_x[1])
    grad_yy = 0.5 * (vnext_y[1] - vprev_y[1])
    grad_zz = -(grad_xx + grad_yy)
    strain_xy = 0.5 * (grad_xy + grad_yx)
    spin_xy = 0.5 * (grad_xy - grad_yx)
    upwind = (
        jnp.maximum(flow_x, 0.0)[:, None, :] * (centre - prev_x)
        + jnp.minimum(flow_x, 0.0)[:, None, :] * (next_x - centre)
        + jnp.maximum(flow_y, 0.0)[:, None, :] * (centre - prev_y)
        + jnp.minimum(flow_y, 0.0)[:, None, :] * (next_y - centre)
    )
    parts = [centre[:, index, :] for index in range(6)]
    orient = [
        [parts[0], parts[3], parts[4]],
        [parts[3], parts[1], parts[5]],
        [parts[4], parts[5], parts[2]],
    ]
    zero = jnp.zeros_like(grad_xx)
    rate = [[grad_xx, strain_xy, zero], [strain_xy, grad_yy, zero], [zero, zero, grad_zz]]
    spin = [[zero, spin_xy, zero], [-spin_xy, zero, zero], [zero, zero, zero]]
    contraction = sum(
        (orient[first][second] * rate[first][second] for first in range(3) for second in range(3))
    )
    shear = jnp.sqrt(
        2.0
        * sum(
            (rate[first][second] * rate[first][second] for first in range(3) for second in range(3))
        )
        + 1.0
    )
    spin_orient = product(spin, orient)
    orient_spin = product(orient, spin)
    rate_orient = product(rate, orient)
    orient_rate = product(orient, rate)
    sources = []
    for first, second in ((0, 0), (1, 1), (2, 2), (0, 1), (0, 2), (1, 2)):
        delta = 1.0 if first == second else 0.0
        sources.append(
            spin_orient[first][second]
            - orient_spin[first][second]
            + shape_factor
            * (
                rate_orient[first][second]
                + orient_rate[first][second]
                - 2.0 * contraction * orient[first][second]
            )
            + 2.0 * interaction * shear * (delta - 3.0 * orient[first][second])
        )
    sources = sources + [grad_xx, grad_yy, strain_xy]
    for first, second in ((0, 0), (1, 1), (0, 1)):
        sources.append(
            2.0
            * shear_modulus
            * (rate[first][second] + fiber_number * contraction * orient[first][second])
        )
    source = jnp.stack(sources, axis=1)
    return centre + time_step * (source - upwind)


def per_device(
    old_states,
    weight_tiles,
    source_block,
    tile_index,
    dest_device,
    dest_block,
    send_count,
    velocity,
):
    slot_count = source_block.shape[0]
    block_count = old_states.shape[0]
    state_count = old_states.shape[1]
    lane_count = old_states.shape[2]
    tile_rows = velocity.shape[1]
    pieces = contributions(old_states, weight_tiles, source_block, tile_index, send_count, dest_block)
    pieces = pieces[:, : state_count + 1]
    is_live = jnp.arange(slot_count) < send_count[0]
    width_y = lax.axis_size("gy")
    width_x = lax.axis_size("gx")
    capacity = slot_count // 4
    own_x = lax.axis_index("gx")
    own_y = lax.axis_index("gy")
    step_x = dest_device // width_y - own_x
    step_y = dest_device % width_y - own_y
    direction = (step_x + 1) * 3 + (step_y + 1)
    matches = ((direction[:, None] == jnp.arange(9)[None, :]) & is_live[:, None]).astype(jnp.int32)
    earlier = jnp.cumsum(matches, axis=0) - matches
    position = jnp.sum(earlier * matches, axis=1)
    target = jnp.where(is_live, direction * capacity + position, 9 * capacity)
    placing = target[None, :] == jnp.arange(9 * capacity)[:, None]
    outgoing = jnp.einsum(
        "ps,scn->cpn", placing.astype(jnp.bfloat16), pieces, preferred_element_type=jnp.float32
    ).astype(jnp.bfloat16)
    channels = state_count + 1
    arrived = []
    for move_x in (-1, 0, 1):
        for move_y in (-1, 0, 1):
            begin = ((move_x + 1) * 3 + (move_y + 1)) * capacity
            chunk = outgoing[:, begin:begin + capacity, :]
            if move_x != 0 or move_y != 0:
                pairs = []
                for source_x in range(width_x):
                    for source_y in range(width_y):
                        goal_x = source_x + move_x
                        goal_y = source_y + move_y
                        if 0 <= goal_x < width_x and 0 <= goal_y < width_y:
                            pairs.append((source_x * width_y + source_y, goal_x * width_y + goal_y))
                chunk = lax.ppermute(chunk, ("gx", "gy"), pairs)
            arrived.append(chunk)
    arrived = jnp.concatenate(arrived, axis=1)
    ids = arrived[state_count, :, 0].astype(jnp.int32)
    selector = (jnp.arange(tile_rows)[:, None] == ids[None, :]).astype(jnp.bfloat16)
    remapped = jnp.einsum(
        "rp,cpn->rcn", selector, arrived[:state_count], preferred_element_type=jnp.float32
    )
    flow_rows = jnp.transpose(velocity, (1, 0, 2))
    both_near = neighbours(jnp.concatenate([remapped, flow_rows], axis=1), 0, 2)
    state_near = tuple(near[:, :state_count] for near in both_near)
    flow_near = tuple(jnp.transpose(near[:, state_count:], (1, 0, 2)) for near in both_near)
    return advance(remapped, state_near, velocity, flow_near)


def solution(mesh):
    in_specs = (
        P(("gx", "gy"), None, None),
        P(("gx", "gy"), None, None),
        P(("gx", "gy")),
        P(("gx", "gy")),
        P(("gx", "gy")),
        P(("gx", "gy")),
        P(("gx", "gy")),
        P(None, "gx", "gy"),
    )
    out_specs = P("gx", None, "gy")
    return jax.shard_map(
        per_device, mesh=mesh, in_specs=in_specs, out_specs=out_specs, check_vma=False
    )
```

```python
import functools

import jax
import jax.numpy as jnp
from jax import lax
from jax.sharding import PartitionSpec as P
from jax.experimental import pallas as pl
from jax.experimental.pallas import tpu as pltpu

time_step = 0.2
shape_factor = 0.95
interaction = 0.01
shear_modulus = 1.0
fiber_number = 2.0


GROUP = 64


def contribution_kernel(
    state_rows, tile_ref, source_ref, count_ref, label_ref, old_ref, weight_hbm, out_ref, weight_buf, sems
):
    step = pl.program_id(0)
    steps = pl.num_programs(0)
    rows = weight_hbm.shape[1]

    def copy(chunk, slot, member):
        tile = tile_ref[chunk * GROUP + member]
        return pltpu.make_async_copy(
            weight_hbm.at[tile],
            weight_buf.at[slot, member // 2, pl.ds((member % 2) * rows, rows)],
            sems.at[slot, member],
        )

    def fetch(chunk, slot):
        for member in range(GROUP):
            copy(chunk, slot, member).start()

    @pl.when(step == 0)
    def _():
        fetch(0, 0)

    @pl.when(step + 1 < steps)
    def _():
        fetch(step + 1, (step + 1) % 2)

    slot = step % 2
    for member in range(GROUP):
        copy(step, slot, member).wait()
    count = count_ref[0]
    padded = old_ref.shape[1]
    states = state_rows
    for pair in range(GROUP // 2):
        first = step * GROUP + 2 * pair
        blocks = jnp.concatenate(
            [old_ref[source_ref[first]], old_ref[source_ref[first + 1]]], axis=0
        )
        both = lax.dot_general(
            blocks, weight_buf[slot, pair], (((1,), (1,)), ((), ())), preferred_element_type=jnp.float32
        )
        for half in range(2):
            index = first + half
            piece = both[half * padded:(half + 1) * padded, half * rows:(half + 1) * rows]
            piece = jnp.where(index < count, piece, 0.0)
            tag = jnp.where(
                lax.broadcasted_iota(jnp.int32, piece.shape, 0) == states,
                label_ref[index].astype(jnp.float32),
                0.0,
            )
            out_ref[2 * pair + half] = (piece + tag).astype(out_ref.dtype)


def contributions(old_states, weight_tiles, source_block, tile_index, send_count, dest_block):
    slot_count = source_block.shape[0]
    block_count, state_count, lane_count = old_states.shape
    rows = weight_tiles.shape[1]
    padded = -(-(state_count + 1) // 16) * 16
    old_padded = jnp.pad(old_states, ((0, 0), (0, padded - state_count), (0, 0)))
    grid_spec = pltpu.PrefetchScalarGridSpec(
        num_scalar_prefetch=4,
        grid=(slot_count // GROUP,),
        in_specs=[
            pl.BlockSpec((block_count, padded, lane_count), lambda i, *_: (0, 0, 0)),
            pl.BlockSpec(memory_space=pl.ANY),
        ],
        out_specs=pl.BlockSpec((GROUP, padded, rows), lambda i, *_: (i, 0, 0)),
        scratch_shapes=[
            pltpu.VMEM((2, GROUP // 2, 2 * rows, weight_tiles.shape[2]), weight_tiles.dtype),
            pltpu.SemaphoreType.DMA((2, GROUP)),
        ],
    )
    return pl.pallas_call(
        functools.partial(contribution_kernel, state_count),
        grid_spec=grid_spec,
        out_shape=jax.ShapeDtypeStruct((slot_count, padded, rows), jnp.bfloat16),
        compiler_params=pltpu.CompilerParams(dimension_semantics=("arbitrary",)),
    )(tile_index, source_block, send_count, dest_block, old_padded, weight_tiles)


def shift_in(value, axis, step):
    count = lax.axis_size(axis)
    pairs = [(source, source + step) for source in range(count) if 0 <= source + step < count]
    return lax.ppermute(value, axis, pairs)


def neighbours(x, dim_x, dim_y):
    length_x = x.shape[dim_x]
    length_y = x.shape[dim_y]
    last_x = lax.slice_in_dim(x, length_x - 1, length_x, axis=dim_x)
    first_x = lax.slice_in_dim(x, 0, 1, axis=dim_x)
    last_y = jnp.moveaxis(lax.index_in_dim(x, length_y - 1, axis=dim_y, keepdims=False), dim_x, -1)
    first_y = jnp.moveaxis(lax.index_in_dim(x, 0, axis=dim_y, keepdims=False), dim_x, -1)
    return assemble(x, dim_x, dim_y, first_x, last_x, first_y, last_y)


def assemble(x, dim_x, dim_y, first_x, last_x, first_y, last_y):
    length_x = x.shape[dim_x]
    length_y = x.shape[dim_y]
    before_x = shift_in(last_x, "gx", 1)
    after_x = shift_in(first_x, "gx", -1)
    before_y = jnp.expand_dims(jnp.moveaxis(shift_in(last_y, "gy", 1), -1, dim_x), dim_y)
    after_y = jnp.expand_dims(jnp.moveaxis(shift_in(first_y, "gy", -1), -1, dim_x), dim_y)
    prev_x = jnp.concatenate([before_x, lax.slice_in_dim(x, 0, length_x - 1, axis=dim_x)], axis=dim_x)
    next_x = jnp.concatenate([lax.slice_in_dim(x, 1, length_x, axis=dim_x), after_x], axis=dim_x)
    prev_y = jnp.concatenate([before_y, lax.slice_in_dim(x, 0, length_y - 1, axis=dim_y)], axis=dim_y)
    next_y = jnp.concatenate([lax.slice_in_dim(x, 1, length_y, axis=dim_y), after_y], axis=dim_y)
    return prev_x, next_x, prev_y, next_y


def product(left, right):
    return [
        [
            sum((left[first][inner] * right[inner][second] for inner in range(3)))
            for second in range(3)
        ]
        for first in range(3)
    ]


def advance(centre, state_near, flow, flow_near):
    prev_x, next_x, prev_y, next_y = state_near
    vprev_x, vnext_x, vprev_y, vnext_y = flow_near
    flow_x = flow[0]
    flow_y = flow[1]
    grad_xx = 0.5 * (vnext_x[0] - vprev_x[0])
    grad_xy = 0.5 * (vnext_y[0] - vprev_y[0])
    grad_yx = 0.5 * (vnext_x[1] - vprev_x[1])
    grad_yy = 0.5 * (vnext_y[1] - vprev_y[1])
    grad_zz = -(grad_xx + grad_yy)
    strain_xy = 0.5 * (grad_xy + grad_yx)
    spin_xy = 0.5 * (grad_xy - grad_yx)
    upwind = (
        jnp.maximum(flow_x, 0.0)[:, None, :] * (centre - prev_x)
        + jnp.minimum(flow_x, 0.0)[:, None, :] * (next_x - centre)
        + jnp.maximum(flow_y, 0.0)[:, None, :] * (centre - prev_y)
        + jnp.minimum(flow_y, 0.0)[:, None, :] * (next_y - centre)
    )
    parts = [centre[:, index, :] for index in range(6)]
    orient = [
        [parts[0], parts[3], parts[4]],
        [parts[3], parts[1], parts[5]],
        [parts[4], parts[5], parts[2]],
    ]
    zero = jnp.zeros_like(grad_xx)
    rate = [[grad_xx, strain_xy, zero], [strain_xy, grad_yy, zero], [zero, zero, grad_zz]]
    spin = [[zero, spin_xy, zero], [-spin_xy, zero, zero], [zero, zero, zero]]
    contraction = sum(
        (orient[first][second] * rate[first][second] for first in range(3) for second in range(3))
    )
    shear = jnp.sqrt(
        2.0
        * sum(
            (rate[first][second] * rate[first][second] for first in range(3) for second in range(3))
        )
        + 1.0
    )
    spin_orient = product(spin, orient)
    orient_spin = product(orient, spin)
    rate_orient = product(rate, orient)
    orient_rate = product(orient, rate)
    sources = []
    for first, second in ((0, 0), (1, 1), (2, 2), (0, 1), (0, 2), (1, 2)):
        delta = 1.0 if first == second else 0.0
        sources.append(
            spin_orient[first][second]
            - orient_spin[first][second]
            + shape_factor
            * (
                rate_orient[first][second]
                + orient_rate[first][second]
                - 2.0 * contraction * orient[first][second]
            )
            + 2.0 * interaction * shear * (delta - 3.0 * orient[first][second])
        )
    sources = sources + [grad_xx, grad_yy, strain_xy]
    for first, second in ((0, 0), (1, 1), (0, 1)):
        sources.append(
            2.0
            * shear_modulus
            * (rate[first][second] + fiber_number * contraction * orient[first][second])
        )
    source = jnp.stack(sources, axis=1)
    return centre + time_step * (source - upwind)


def per_device(
    old_states,
    weight_tiles,
    source_block,
    tile_index,
    dest_device,
    dest_block,
    send_count,
    velocity,
):
    slot_count = source_block.shape[0]
    block_count = old_states.shape[0]
    state_count = old_states.shape[1]
    lane_count = old_states.shape[2]
    tile_rows = velocity.shape[1]
    pieces = contributions(old_states, weight_tiles, source_block, tile_index, send_count, dest_block)
    pieces = pieces[:, : state_count + 1]
    is_live = jnp.arange(slot_count) < send_count[0]
    width_y = lax.axis_size("gy")
    width_x = lax.axis_size("gx")
    capacity = slot_count // 4
    own_x = lax.axis_index("gx")
    own_y = lax.axis_index("gy")
    step_x = dest_device // width_y - own_x
    step_y = dest_device % width_y - own_y
    direction = (step_x + 1) * 3 + (step_y + 1)
    matches = ((direction[:, None] == jnp.arange(9)[None, :]) & is_live[:, None]).astype(jnp.int32)
    earlier = jnp.cumsum(matches, axis=0) - matches
    position = jnp.sum(earlier * matches, axis=1)
    target = jnp.where(is_live, direction * capacity + position, 9 * capacity)
    placing = target[None, :] == jnp.arange(9 * capacity)[:, None]
    placing = placing.astype(jnp.bfloat16)
    arrived = []
    for move_x in (-1, 0, 1):
        for move_y in (-1, 0, 1):
            begin = ((move_x + 1) * 3 + (move_y + 1)) * capacity
            chunk = jnp.einsum(
                "ps,scn->cpn",
                placing[begin:begin + capacity],
                pieces,
                preferred_element_type=jnp.float32,
            ).astype(jnp.bfloat16)
            if move_x != 0 or move_y != 0:
                pairs = []
                for source_x in range(width_x):
                    for source_y in range(width_y):
                        goal_x = source_x + move_x
                        goal_y = source_y + move_y
                        if 0 <= goal_x < width_x and 0 <= goal_y < width_y:
                            pairs.append((source_x * width_y + source_y, goal_x * width_y + goal_y))
                chunk = lax.ppermute(chunk, ("gx", "gy"), pairs)
            arrived.append(chunk)
    arrived = jnp.concatenate(arrived, axis=1)
    ids = arrived[state_count, :, 0].astype(jnp.int32)
    selector = (jnp.arange(tile_rows)[:, None] == ids[None, :]).astype(jnp.bfloat16)
    remapped = jnp.einsum(
        "rp,cpn->rcn", selector, arrived[:state_count], preferred_element_type=jnp.float32
    )
    flow_rows = jnp.transpose(velocity, (1, 0, 2))
    both_near = neighbours(jnp.concatenate([remapped, flow_rows], axis=1), 0, 2)
    state_near = tuple(near[:, :state_count] for near in both_near)
    flow_near = tuple(jnp.transpose(near[:, state_count:], (1, 0, 2)) for near in both_near)
    return advance(remapped, state_near, velocity, flow_near)


def solution(mesh):
    in_specs = (
        P(("gx", "gy"), None, None),
        P(("gx", "gy"), None, None),
        P(("gx", "gy")),
        P(("gx", "gy")),
        P(("gx", "gy")),
        P(("gx", "gy")),
        P(("gx", "gy")),
        P(None, "gx", "gy"),
    )
    out_specs = P("gx", None, "gy")
    return jax.shard_map(
        per_device, mesh=mesh, in_specs=in_specs, out_specs=out_specs, check_vma=False
    )
```

```python
import functools

import jax
import jax.numpy as jnp
from jax import lax
from jax.sharding import PartitionSpec as P
from jax.experimental import pallas as pl
from jax.experimental.pallas import tpu as pltpu

time_step = 0.2
shape_factor = 0.95
interaction = 0.01
shear_modulus = 1.0
fiber_number = 2.0


GROUP = 64


def contribution_kernel(
    state_rows, tile_ref, source_ref, count_ref, label_ref, old_ref, weight_hbm, out_ref, weight_buf, sems
):
    step = pl.program_id(0)
    steps = pl.num_programs(0)
    rows = weight_hbm.shape[1]

    def copy(chunk, slot, member):
        tile = tile_ref[chunk * GROUP + member]
        return pltpu.make_async_copy(
            weight_hbm.at[tile],
            weight_buf.at[slot, member // 2, pl.ds((member % 2) * rows, rows)],
            sems.at[slot, member],
        )

    def fetch(chunk, slot):
        for member in range(GROUP):
            copy(chunk, slot, member).start()

    @pl.when(step == 0)
    def _():
        fetch(0, 0)

    @pl.when(step + 1 < steps)
    def _():
        fetch(step + 1, (step + 1) % 2)

    slot = step % 2
    for member in range(GROUP):
        copy(step, slot, member).wait()
    count = count_ref[0]
    padded = old_ref.shape[1]
    states = state_rows
    for pair in range(GROUP // 2):
        first = step * GROUP + 2 * pair
        blocks = jnp.concatenate(
            [old_ref[source_ref[first]], old_ref[source_ref[first + 1]]], axis=0
        )
        both = lax.dot_general(
            blocks, weight_buf[slot, pair], (((1,), (1,)), ((), ())), preferred_element_type=jnp.float32
        )
        for half in range(2):
            index = first + half
            piece = both[half * padded:(half + 1) * padded, half * rows:(half + 1) * rows]
            piece = jnp.where(index < count, piece, 0.0)
            tag = jnp.where(
                lax.broadcasted_iota(jnp.int32, piece.shape, 0) == states,
                label_ref[index].astype(jnp.float32),
                0.0,
            )
            out_ref[2 * pair + half] = (piece + tag).astype(out_ref.dtype)


def contributions(old_states, weight_tiles, source_block, tile_index, send_count, dest_block):
    slot_count = source_block.shape[0]
    block_count, state_count, lane_count = old_states.shape
    rows = weight_tiles.shape[1]
    padded = -(-(state_count + 1) // 16) * 16
    old_padded = jnp.pad(old_states, ((0, 0), (0, padded - state_count), (0, 0)))
    grid_spec = pltpu.PrefetchScalarGridSpec(
        num_scalar_prefetch=4,
        grid=(slot_count // GROUP,),
        in_specs=[
            pl.BlockSpec((block_count, padded, lane_count), lambda i, *_: (0, 0, 0)),
            pl.BlockSpec(memory_space=pl.ANY),
        ],
        out_specs=pl.BlockSpec((GROUP, padded, rows), lambda i, *_: (i, 0, 0)),
        scratch_shapes=[
            pltpu.VMEM((2, GROUP // 2, 2 * rows, weight_tiles.shape[2]), weight_tiles.dtype),
            pltpu.SemaphoreType.DMA((2, GROUP)),
        ],
    )
    return pl.pallas_call(
        functools.partial(contribution_kernel, state_count),
        grid_spec=grid_spec,
        out_shape=jax.ShapeDtypeStruct((slot_count, padded, rows), jnp.bfloat16),
        compiler_params=pltpu.CompilerParams(dimension_semantics=("arbitrary",)),
    )(tile_index, source_block, send_count, dest_block, old_padded, weight_tiles)


def shift_in(value, axis, step):
    count = lax.axis_size(axis)
    pairs = [(source, source + step) for source in range(count) if 0 <= source + step < count]
    return lax.ppermute(value, axis, pairs)


def neighbours(x, dim_x, dim_y):
    length_x = x.shape[dim_x]
    length_y = x.shape[dim_y]
    last_x = lax.slice_in_dim(x, length_x - 1, length_x, axis=dim_x)
    first_x = lax.slice_in_dim(x, 0, 1, axis=dim_x)
    last_y = jnp.moveaxis(lax.index_in_dim(x, length_y - 1, axis=dim_y, keepdims=False), dim_x, -1)
    first_y = jnp.moveaxis(lax.index_in_dim(x, 0, axis=dim_y, keepdims=False), dim_x, -1)
    return assemble(x, dim_x, dim_y, first_x, last_x, first_y, last_y)


def assemble(x, dim_x, dim_y, first_x, last_x, first_y, last_y):
    length_x = x.shape[dim_x]
    length_y = x.shape[dim_y]
    before_x = shift_in(last_x, "gx", 1)
    after_x = shift_in(first_x, "gx", -1)
    before_y = jnp.expand_dims(jnp.moveaxis(shift_in(last_y, "gy", 1), -1, dim_x), dim_y)
    after_y = jnp.expand_dims(jnp.moveaxis(shift_in(first_y, "gy", -1), -1, dim_x), dim_y)
    prev_x = jnp.concatenate([before_x, lax.slice_in_dim(x, 0, length_x - 1, axis=dim_x)], axis=dim_x)
    next_x = jnp.concatenate([lax.slice_in_dim(x, 1, length_x, axis=dim_x), after_x], axis=dim_x)
    prev_y = jnp.concatenate([before_y, lax.slice_in_dim(x, 0, length_y - 1, axis=dim_y)], axis=dim_y)
    next_y = jnp.concatenate([lax.slice_in_dim(x, 1, length_y, axis=dim_y), after_y], axis=dim_y)
    return prev_x, next_x, prev_y, next_y


def product(left, right):
    return [
        [
            sum((left[first][inner] * right[inner][second] for inner in range(3)))
            for second in range(3)
        ]
        for first in range(3)
    ]


def advance(centre, state_near, flow, flow_near):
    prev_x, next_x, prev_y, next_y = state_near
    vprev_x, vnext_x, vprev_y, vnext_y = flow_near
    flow_x = flow[0]
    flow_y = flow[1]
    grad_xx = 0.5 * (vnext_x[0] - vprev_x[0])
    grad_xy = 0.5 * (vnext_y[0] - vprev_y[0])
    grad_yx = 0.5 * (vnext_x[1] - vprev_x[1])
    grad_yy = 0.5 * (vnext_y[1] - vprev_y[1])
    grad_zz = -(grad_xx + grad_yy)
    strain_xy = 0.5 * (grad_xy + grad_yx)
    spin_xy = 0.5 * (grad_xy - grad_yx)
    upwind = (
        jnp.maximum(flow_x, 0.0)[:, None, :] * (centre - prev_x)
        + jnp.minimum(flow_x, 0.0)[:, None, :] * (next_x - centre)
        + jnp.maximum(flow_y, 0.0)[:, None, :] * (centre - prev_y)
        + jnp.minimum(flow_y, 0.0)[:, None, :] * (next_y - centre)
    )
    parts = [centre[:, index, :] for index in range(6)]
    orient = [
        [parts[0], parts[3], parts[4]],
        [parts[3], parts[1], parts[5]],
        [parts[4], parts[5], parts[2]],
    ]
    zero = jnp.zeros_like(grad_xx)
    rate = [[grad_xx, strain_xy, zero], [strain_xy, grad_yy, zero], [zero, zero, grad_zz]]
    spin = [[zero, spin_xy, zero], [-spin_xy, zero, zero], [zero, zero, zero]]
    contraction = sum(
        (orient[first][second] * rate[first][second] for first in range(3) for second in range(3))
    )
    shear = jnp.sqrt(
        2.0
        * sum(
            (rate[first][second] * rate[first][second] for first in range(3) for second in range(3))
        )
        + 1.0
    )
    spin_orient = product(spin, orient)
    orient_spin = product(orient, spin)
    rate_orient = product(rate, orient)
    orient_rate = product(orient, rate)
    sources = []
    for first, second in ((0, 0), (1, 1), (2, 2), (0, 1), (0, 2), (1, 2)):
        delta = 1.0 if first == second else 0.0
        sources.append(
            spin_orient[first][second]
            - orient_spin[first][second]
            + shape_factor
            * (
                rate_orient[first][second]
                + orient_rate[first][second]
                - 2.0 * contraction * orient[first][second]
            )
            + 2.0 * interaction * shear * (delta - 3.0 * orient[first][second])
        )
    sources = sources + [grad_xx, grad_yy, strain_xy]
    for first, second in ((0, 0), (1, 1), (0, 1)):
        sources.append(
            2.0
            * shear_modulus
            * (rate[first][second] + fiber_number * contraction * orient[first][second])
        )
    source = jnp.stack(sources, axis=1)
    return centre + time_step * (source - upwind)


def per_device(
    old_states,
    weight_tiles,
    source_block,
    tile_index,
    dest_device,
    dest_block,
    send_count,
    velocity,
):
    slot_count = source_block.shape[0]
    block_count = old_states.shape[0]
    state_count = old_states.shape[1]
    lane_count = old_states.shape[2]
    tile_rows = velocity.shape[1]
    pieces = contributions(old_states, weight_tiles, source_block, tile_index, send_count, dest_block)
    pieces = pieces[:, : state_count + 1]
    is_live = jnp.arange(slot_count) < send_count[0]
    width_y = lax.axis_size("gy")
    width_x = lax.axis_size("gx")
    capacity = slot_count // 4
    own_x = lax.axis_index("gx")
    own_y = lax.axis_index("gy")
    step_x = dest_device // width_y - own_x
    step_y = dest_device % width_y - own_y
    direction = (step_x + 1) * 3 + (step_y + 1)
    matches = ((direction[:, None] == jnp.arange(9)[None, :]) & is_live[:, None]).astype(jnp.int32)
    earlier = jnp.cumsum(matches, axis=0) - matches
    position = jnp.sum(earlier * matches, axis=1)
    target = jnp.where(is_live, direction * capacity + position, 9 * capacity)
    placing = target[None, :] == jnp.arange(9 * capacity)[:, None]
    placing = placing.astype(jnp.bfloat16)
    arrived = []
    moves = [(x, y) for x in (-1, 0, 1) for y in (-1, 0, 1) if x != 0 or y != 0] + [(0, 0)]
    for move_x, move_y in moves:
        if True:
            begin = ((move_x + 1) * 3 + (move_y + 1)) * capacity
            chunk = jnp.einsum(
                "ps,scn->cpn",
                placing[begin:begin + capacity],
                pieces,
                preferred_element_type=jnp.float32,
            ).astype(jnp.bfloat16)
            if move_x != 0 or move_y != 0:
                pairs = []
                for source_x in range(width_x):
                    for source_y in range(width_y):
                        goal_x = source_x + move_x
                        goal_y = source_y + move_y
                        if 0 <= goal_x < width_x and 0 <= goal_y < width_y:
                            pairs.append((source_x * width_y + source_y, goal_x * width_y + goal_y))
                chunk = lax.ppermute(chunk, ("gx", "gy"), pairs)
            arrived.append(chunk)
    arrived = jnp.concatenate(arrived, axis=1)
    ids = arrived[state_count, :, 0].astype(jnp.int32)
    selector = (jnp.arange(tile_rows)[:, None] == ids[None, :]).astype(jnp.bfloat16)
    remapped = jnp.einsum(
        "rp,cpn->rcn", selector, arrived[:state_count], preferred_element_type=jnp.float32
    )
    flow_rows = jnp.transpose(velocity, (1, 0, 2))
    both_near = neighbours(jnp.concatenate([remapped, flow_rows], axis=1), 0, 2)
    state_near = tuple(near[:, :state_count] for near in both_near)
    flow_near = tuple(jnp.transpose(near[:, state_count:], (1, 0, 2)) for near in both_near)
    return advance(remapped, state_near, velocity, flow_near)


def solution(mesh):
    in_specs = (
        P(("gx", "gy"), None, None),
        P(("gx", "gy"), None, None),
        P(("gx", "gy")),
        P(("gx", "gy")),
        P(("gx", "gy")),
        P(("gx", "gy")),
        P(("gx", "gy")),
        P(None, "gx", "gy"),
    )
    out_specs = P("gx", None, "gy")
    return jax.shard_map(
        per_device, mesh=mesh, in_specs=in_specs, out_specs=out_specs, check_vma=False
    )
```
